128 devices in a mesh: batch: 8 (over y, core), seq: 16 (over x, z).
Axes of the slice: x: 4, y: 4, z: 4, core: 2. Of those that a mesh axis runs over, the one named last changes fastest.
Arguments:
- frames: bfloat16 [8, 3072, 1024], P('batch', 'seq'), may hold values from -6 to 6
- lengths: int32 [8], P('batch'), may hold values from 768 to 3072, as said below
- w_qkv: bfloat16 [1024, 3072], replicated, may hold values from -0.25 to 0.25
- w_out: bfloat16 [1024, 1024], replicated, may hold values from -0.1875 to 0.1875
- cotangent: bfloat16 [8, 3072, 1024], P('batch', 'seq'), may hold values from -6 to 6
Outputs:
- output: bfloat16 [8, 3072, 1024], P('batch', 'seq')
- grad_input: bfloat16 [8, 3072, 1024], P('batch', 'seq')
- grad_qkv: float32 [1024, 3072], P('seq')
- grad_out: float32 [1024, 1024], P('seq')
The draws below stay inside these ranges and needn't reach their ends.
Inputs may be any that keep to these rules, and one draw needn't show every extreme that they name: `lengths`: at least one utterance has all 3072 frames valid.
All inputs are finite; a program needn't handle non-finite values.
Results may differ from the reference program's by a relative error of at most 0.012.
The reference program's roundings to bfloat16 on the way count: a program that leaves them out, or rounds other values in their place, can miss the bound.
Values may be sent and summed in bfloat16 or wider, within the bound.
No kernel may reach another device: no remote copies, remote signals or barrier semaphores. Data moves between devices by JAX's collectives and lax.ppermute only.
A program may use at most 128 MiB of HBM per device.

```python
import jax
import jax.numpy as jnp
from jax import lax

D = 1024
H = 8
HD = 128
FRAMES = 3072
UTTS = 8


def draw_lengths(key, part):
    first, second = jax.random.split(key)
    drawn = jax.random.randint(first, (UTTS,), FRAMES // 4, FRAMES + 1)
    chosen = jax.random.randint(second, (), 0, UTTS)
    return jnp.where(jnp.arange(UTTS) == chosen, FRAMES, drawn).astype(jnp.int32)


def draw_w_qkv(key, part):
    first = jax.random.fold_in(key, 0)
    spread = float(D) ** (-0.5)
    entries = jnp.clip(jax.random.normal(first, (D, 3 * D), jnp.float32), -6.0, 6.0) * spread
    entries = jnp.clip(entries, -0.25, 0.25)
    return entries.astype(jnp.bfloat16)


def block_scale(own_key, extent, shards, low, high):
    factor_of = 1.0
    for dim, shards_of in shards:
        draws = jax.random.uniform(jax.random.fold_in(jax.random.fold_in(own_key, 6), dim), (shards_of,), jnp.float32, low / len(shards), high / len(shards))
        factor_of = factor_of * jnp.repeat(jnp.exp(draws), extent[dim] // shards_of).reshape((-1,) + (1,) * (len(extent) - 1 - dim))
    return factor_of


def gaussian(rng, shape, deviation, limit, cuts=(), held_as=jnp.bfloat16):
    gain = block_scale(rng, shape, cuts, -0.22, 0.18) if cuts else 1.0
    array = jax.random.normal(rng, shape, jnp.float32) * deviation * gain
    return jnp.minimum(jnp.maximum(array, -limit), limit).astype(held_as)


def setup_inputs(seed: int = 0) -> dict:
    splits = jax.random.split(jax.random.key(seed), 6)
    frames = gaussian(splits[0], (UTTS, FRAMES, D), 1.0, 6.0, ((0, 8), (1, 16)))
    lengths = draw_lengths(jax.random.fold_in(splits[5], 71), 0)
    w_qkv = draw_w_qkv(jax.random.fold_in(splits[5], 71), 0)
    w_out = gaussian(splits[3], (D, D), D ** -0.5, 0.1875)
    cotangent = gaussian(splits[4], (UTTS, FRAMES, D), 1.0, 6.0, ((0, 8), (1, 16)))
    return dict(frames=frames, lengths=lengths, w_qkv=w_qkv, w_out=w_out, cotangent=cotangent)


def layer_norm(values):
    mean = lax.optimization_barrier(jnp.mean(values, axis=-1, keepdims=True))
    centred = values - mean
    var = lax.optimization_barrier(jnp.mean(centred * centred, axis=-1, keepdims=True))
    return centred * lax.rsqrt(var + 1e-05)

def block_forward(query_rows, keys, values, bias, scale):
    scores = jnp.dot(query_rows, keys.T, preferred_element_type=jnp.float32) * scale + bias[None, :]
    top = lax.optimization_barrier(jnp.max(scores, axis=1, keepdims=True))
    expo = jnp.exp(scores - top)
    probs = expo / lax.optimization_barrier(jnp.sum(expo, axis=1, keepdims=True))
    p_half = probs.astype(jnp.bfloat16)
    return (probs, p_half, jnp.dot(p_half, values, preferred_element_type=jnp.float32))

def head_forward(query, keys, values, bias, scale):
    total = query.shape[0]
    rows = min(512, total)
    blocks = query.reshape(total // rows, rows, query.shape[1])

    def one_block(query_rows):
        return block_forward(query_rows, keys, values, bias, scale)[2].astype(jnp.bfloat16)
    return lax.map(one_block, blocks).reshape(total, query.shape[1])

def head_backward(query, keys, values, dcontext, bias, scale):
    total, width = query.shape
    rows = min(512, total)
    qblocks = query.reshape(total // rows, rows, width)
    dblocks = dcontext.reshape(total // rows, rows, width)

    def step(carry, item):
        dkeys, dvalues = carry
        query_rows, d_rows = item
        probs, p_half, unused = block_forward(query_rows, keys, values, bias, scale)
        dprobs = jnp.dot(d_rows, values.T, preferred_element_type=jnp.float32)
        delta = lax.optimization_barrier(jnp.sum(probs * dprobs, axis=1, keepdims=True))
        dscores = (probs * (dprobs - delta)).astype(jnp.bfloat16)
        dquery = jnp.dot(dscores, keys, preferred_element_type=jnp.float32) * scale
        dkeys = dkeys + jnp.dot(dscores.T, query_rows, preferred_element_type=jnp.float32) * scale
        dvalues = dvalues + jnp.dot(p_half.T, d_rows, preferred_element_type=jnp.float32)
        return ((dkeys, dvalues), dquery.astype(jnp.bfloat16))
    start = (jnp.zeros((total, width), jnp.float32), jnp.zeros((total, width), jnp.float32))
    (dkeys, dvalues), dquery = lax.scan(step, start, (qblocks, dblocks))
    return (dquery.reshape(total, width), dkeys.astype(jnp.bfloat16), dvalues.astype(jnp.bfloat16))

def reference(frames, lengths, w_qkv, w_out, cotangent):
    scale = float(HD) ** (-0.5)
    inputs = frames.astype(jnp.float32)
    normed = layer_norm(inputs).astype(jnp.bfloat16)
    normed_rows = normed.reshape(UTTS * FRAMES, D)
    qkv = jnp.dot(normed_rows, w_qkv, preferred_element_type=jnp.float32).astype(jnp.bfloat16)
    qkv = qkv.reshape(UTTS, FRAMES, 3, H, HD)
    position = jnp.arange(FRAMES, dtype=jnp.int32)
    valid = (position[None, :] < lengths[:, None]).astype(jnp.float32)
    grad_rows = (cotangent.astype(jnp.float32) * valid[:, :, None]).astype(jnp.bfloat16).reshape(UTTS * FRAMES, D)
    dcontext = jnp.dot(grad_rows, w_out.T, preferred_element_type=jnp.float32).astype(jnp.bfloat16)
    dcontext = dcontext.reshape(UTTS, FRAMES, H, HD)

    def utterance(item):
        qkv_one, dctx_one, length = item
        bias = jnp.where(position < length, 0.0, -1000000000.0).astype(jnp.float32)
        per_head = qkv_one.transpose(2, 1, 0, 3)
        dper_head = dctx_one.transpose(1, 0, 2)

        def head(pair):
            trio, d_head = pair
            context = head_forward(trio[0], trio[1], trio[2], bias, scale)
            dquery, dkeys, dvalues = head_backward(trio[0], trio[1], trio[2], d_head, bias, scale)
            return (context, jnp.stack([dquery, dkeys, dvalues]))
        context, dtrio = lax.map(head, (per_head, dper_head))
        return (context.transpose(1, 0, 2), dtrio.transpose(2, 1, 0, 3))
    context, dqkv = lax.map(utterance, (qkv, dcontext, lengths))
    context_rows = context.reshape(UTTS * FRAMES, D)
    branch = jnp.dot(context_rows, w_out, preferred_element_type=jnp.float32).reshape(UTTS, FRAMES, D)
    output = (inputs + valid[:, :, None] * branch).astype(jnp.bfloat16)
    grad_out = jnp.dot(context_rows.T, grad_rows, preferred_element_type=jnp.float32)
    dqkv_rows = dqkv.reshape(UTTS * FRAMES, 3 * D)
    grad_qkv = jnp.dot(normed_rows.T, dqkv_rows, preferred_element_type=jnp.float32)
    dnormed = jnp.dot(dqkv_rows, w_qkv.T, preferred_element_type=jnp.float32).reshape(UTTS, FRAMES, D)
    unused, pull = jax.vjp(layer_norm, inputs)
    grad_input = (cotangent.astype(jnp.float32) + pull(dnormed)[0]).astype(jnp.bfloat16)
    return (output, grad_input, grad_qkv, grad_out)
```

```python
import jax
import jax.numpy as jnp
from jax import lax
from jax.sharding import PartitionSpec as P

H = 8


def from_partner(array, axis, stride):
    return lax.ppermute(array, axis, [(i, i ^ 1 << stride) for i in range(lax.axis_size(axis))])


def layer_norm(values):
    mean = jnp.mean(values, axis=-1, keepdims=True)
    centred = values - mean
    var = jnp.mean(centred * centred, axis=-1, keepdims=True)
    return centred * lax.rsqrt(var + 1e-05)


def head_pass(query, keys, values, dcontext, bias, scale):
    total, width = query.shape
    rows = min(512, total)
    qblocks = query.reshape(total // rows, rows, width)
    dblocks = dcontext.reshape(total // rows, rows, width)
    key_count = keys.shape[0]

    def step(carry, item):
        dkeys, dvalues = carry
        query_rows, d_rows = item
        scores = jnp.dot(query_rows, keys.T, preferred_element_type=jnp.float32) * scale + bias[None, :]
        top = jnp.max(scores, axis=1, keepdims=True)
        expo = jnp.exp(scores - top)
        probs = expo / jnp.sum(expo, axis=1, keepdims=True)
        p_half = probs.astype(jnp.bfloat16)
        context = jnp.dot(p_half, values, preferred_element_type=jnp.float32).astype(jnp.bfloat16)
        dprobs = jnp.dot(d_rows, values.T, preferred_element_type=jnp.float32)
        delta = jnp.sum(probs * dprobs, axis=1, keepdims=True)
        dscores = (probs * (dprobs - delta)).astype(jnp.bfloat16)
        dquery = jnp.dot(dscores, keys, preferred_element_type=jnp.float32) * scale
        dkeys = dkeys + jnp.dot(dscores.T, query_rows, preferred_element_type=jnp.float32) * scale
        dvalues = dvalues + jnp.dot(p_half.T, d_rows, preferred_element_type=jnp.float32)
        return ((dkeys, dvalues), (context, dquery.astype(jnp.bfloat16)))

    start = (jnp.zeros((key_count, width), jnp.float32), jnp.zeros((key_count, width), jnp.float32))
    (dkeys, dvalues), (context, dquery) = lax.scan(step, start, (qblocks, dblocks))
    return context.reshape(total, width), dquery.reshape(total, width), dkeys, dvalues


def per_device(frames, lengths, w_qkv, w_out, cotangent):
    width = w_out.shape[0]
    head_size = width // H
    scale = float(head_size) ** (-0.5)
    tok_rows = frames.shape[1]
    seq_count = lax.axis_size("seq")
    groups = seq_count // H
    part_rows = tok_rows // groups
    frame_total = tok_rows * seq_count
    group_index = lax.axis_index("seq") % groups
    length = lengths[0]
    inputs = frames[0].astype(jnp.float32)
    normed = layer_norm(inputs).astype(jnp.bfloat16)
    qkv = jnp.dot(normed, w_qkv, preferred_element_type=jnp.float32).astype(jnp.bfloat16)
    qkv_local = qkv.reshape(tok_rows, 3, H, head_size)
    offset = lax.axis_index("seq") * tok_rows
    own_pos = offset + jnp.arange(tok_rows, dtype=jnp.int32)
    valid = (own_pos < length).astype(jnp.float32)
    grad_rows = (cotangent[0].astype(jnp.float32) * valid[:, None]).astype(jnp.bfloat16)
    dcontext = jnp.dot(grad_rows, w_out.T, preferred_element_type=jnp.float32).astype(jnp.bfloat16)

    qd = jnp.stack([qkv_local[:, 0], dcontext.reshape(tok_rows, H, head_size)], axis=1)
    qd_send = (
        qd.reshape(groups, part_rows, 2, H, head_size)
        .transpose(3, 0, 1, 2, 4)
        .reshape(seq_count, part_rows, 2, head_size)
    )
    paired = qkv_local[:, 1:].transpose(2, 0, 1, 3)
    paired_send = jnp.broadcast_to(paired[:, None], (H, groups, tok_rows, 2, head_size))
    paired_send = paired_send.reshape(seq_count, tok_rows, 2, head_size)
    qd_recv = lax.all_to_all(qd_send, "seq", split_axis=0, concat_axis=0, tiled=True)
    paired_recv = lax.all_to_all(paired_send, "seq", split_axis=0, concat_axis=0, tiled=True)
    queries = qd_recv[:, :, 0].reshape(seq_count * part_rows, head_size)
    dcontext_heads = qd_recv[:, :, 1].reshape(seq_count * part_rows, head_size)
    keys = paired_recv[:, :, 0].reshape(frame_total, head_size)
    values = paired_recv[:, :, 1].reshape(frame_total, head_size)
    position = jnp.arange(frame_total, dtype=jnp.int32)
    bias = jnp.where(position < length, 0.0, -1000000000.0).astype(jnp.float32)

    context_h, dquery, dkeys, dvalues = head_pass(queries, keys, values, dcontext_heads, bias, scale)

    context_back = lax.all_to_all(
        context_h.reshape(seq_count, part_rows, head_size), "seq", split_axis=0, concat_axis=0, tiled=True
    )
    context = (
        context_back.reshape(H, groups, part_rows, head_size).transpose(1, 2, 0, 3).reshape(tok_rows, width)
    )
    branch = jnp.dot(context, w_out, preferred_element_type=jnp.float32)
    output = (inputs + valid[:, None] * branch).astype(jnp.bfloat16)
    out_share = lax.psum_scatter(
        jnp.dot(context.T, grad_rows, preferred_element_type=jnp.float32),
        "seq",
        scatter_dimension=0,
        tiled=True,
    )

    split_grads = jnp.stack([dkeys, dvalues], axis=1).reshape(seq_count, groups, part_rows, 2, head_size)
    own_half = lax.dynamic_index_in_dim(split_grads, group_index, 1, keepdims=False)
    other_half = lax.dynamic_index_in_dim(split_grads, 1 - group_index, 1, keepdims=False)
    partner_half = from_partner(other_half, "seq", 0)
    paired_rows = (own_half + partner_half).astype(jnp.bfloat16)
    dtrio = jnp.concatenate([dquery.reshape(seq_count, part_rows, 1, head_size), paired_rows], axis=2)
    returned_grads = lax.all_to_all(dtrio, "seq", split_axis=0, concat_axis=0, tiled=True)
    dqkv = returned_grads.reshape(H, groups, part_rows, 3, head_size)
    dqkv = dqkv.transpose(1, 2, 3, 0, 4).reshape(tok_rows, 3 * width)
    qkv_share = lax.psum_scatter(
        jnp.dot(normed.T, dqkv, preferred_element_type=jnp.float32),
        "seq",
        scatter_dimension=0,
        tiled=True,
    )
    grad_qkv, grad_out = lax.psum((qkv_share, out_share), "batch")
    dnormed = jnp.dot(dqkv, w_qkv.T, preferred_element_type=jnp.float32)
    unused, pull = jax.vjp(layer_norm, inputs)
    grad_input = (cotangent[0].astype(jnp.float32) + pull(dnormed)[0]).astype(jnp.bfloat16)
    return (output[None], grad_input[None], grad_qkv, grad_out)


def solution(mesh):
    return jax.shard_map(
        per_device,
        mesh=mesh,
        in_specs=(P("batch", "seq", None), P("batch"), P(), P(), P("batch", "seq", None)),
        out_specs=(
            P("batch", "seq", None),
            P("batch", "seq", None),
            P("seq", None),
            P("seq", None),
        ),
        check_vma=False,
    )
```

```python
import jax
import jax.numpy as jnp
from jax import lax
from jax.sharding import PartitionSpec as P
from jax.experimental import pallas as pl
from jax.experimental.pallas import tpu as pltpu
import functools

H = 8


def from_partner(array, axis, stride):
    return lax.ppermute(array, axis, [(i, i ^ 1 << stride) for i in range(lax.axis_size(axis))])


def layer_norm(values):
    mean = jnp.mean(values, axis=-1, keepdims=True)
    centred = values - mean
    var = jnp.mean(centred * centred, axis=-1, keepdims=True)
    return centred * lax.rsqrt(var + 1e-05)


def _attn_kernel(q_ref, do_ref, k_ref, v_ref, bias_ref, ctx_ref, dq_ref, dk_ref, dv_ref, *, scale):
    i = pl.program_id(0)

    @pl.when(i == 0)
    def _():
        dk_ref[...] = jnp.zeros_like(dk_ref)
        dv_ref[...] = jnp.zeros_like(dv_ref)

    q = q_ref[...]
    do = do_ref[...]
    k = k_ref[...]
    v = v_ref[...]
    nt = (((1,), (1,)), ((), ()))
    tn = (((0,), (0,)), ((), ()))
    s = lax.dot_general(q, k, nt, preferred_element_type=jnp.float32) * scale + bias_ref[...]
    m = jnp.max(s, axis=1, keepdims=True)
    e = jnp.exp(s - m)
    p = e / jnp.sum(e, axis=1, keepdims=True)
    p16 = p.astype(jnp.bfloat16)
    ctx_ref[...] = jnp.dot(p16, v, preferred_element_type=jnp.float32).astype(ctx_ref.dtype)
    dp = lax.dot_general(do, v, nt, preferred_element_type=jnp.float32)
    delta = jnp.sum(p * dp, axis=1, keepdims=True)
    ds = (p * (dp - delta)).astype(jnp.bfloat16)
    dq_ref[...] = (jnp.dot(ds, k, preferred_element_type=jnp.float32) * scale).astype(dq_ref.dtype)
    dk_ref[...] += lax.dot_general(ds, q, tn, preferred_element_type=jnp.float32) * scale
    dv_ref[...] += lax.dot_general(p16, do, tn, preferred_element_type=jnp.float32)


def attn_pass(query, keys, values, dcontext, bias, scale, block=256, interpret=False):
    nq, hd = query.shape
    nk = keys.shape[0]
    grid = (nq // block,)
    kernel = functools.partial(_attn_kernel, scale=scale)
    return pl.pallas_call(
        kernel,
        grid=grid,
        in_specs=[
            pl.BlockSpec((block, hd), lambda i: (i, 0)),
            pl.BlockSpec((block, hd), lambda i: (i, 0)),
            pl.BlockSpec((nk, hd), lambda i: (0, 0)),
            pl.BlockSpec((nk, hd), lambda i: (0, 0)),
            pl.BlockSpec((1, nk), lambda i: (0, 0)),
        ],
        out_specs=[
            pl.BlockSpec((block, hd), lambda i: (i, 0)),
            pl.BlockSpec((block, hd), lambda i: (i, 0)),
            pl.BlockSpec((nk, hd), lambda i: (0, 0)),
            pl.BlockSpec((nk, hd), lambda i: (0, 0)),
        ],
        out_shape=[
            jax.ShapeDtypeStruct((nq, hd), jnp.bfloat16),
            jax.ShapeDtypeStruct((nq, hd), jnp.bfloat16),
            jax.ShapeDtypeStruct((nk, hd), jnp.float32),
            jax.ShapeDtypeStruct((nk, hd), jnp.float32),
        ],
        compiler_params=pltpu.CompilerParams(dimension_semantics=("arbitrary",)),
        interpret=interpret,
    )(query, dcontext, keys, values, bias.reshape(1, nk))


def per_device(frames, lengths, w_qkv, w_out, cotangent):
    width = w_out.shape[0]
    head_size = width // H
    scale = float(head_size) ** (-0.5)
    tok_rows = frames.shape[1]
    seq_count = lax.axis_size("seq")
    groups = seq_count // H
    part_rows = tok_rows // groups
    frame_total = tok_rows * seq_count
    group_index = lax.axis_index("seq") % groups
    length = lengths[0]
    inputs = frames[0].astype(jnp.float32)
    normed = layer_norm(inputs).astype(jnp.bfloat16)
    qkv = jnp.dot(normed, w_qkv, preferred_element_type=jnp.float32).astype(jnp.bfloat16)
    qkv_local = qkv.reshape(tok_rows, 3, H, head_size)
    offset = lax.axis_index("seq") * tok_rows
    own_pos = offset + jnp.arange(tok_rows, dtype=jnp.int32)
    valid = (own_pos < length).astype(jnp.float32)
    grad_rows = (cotangent[0].astype(jnp.float32) * valid[:, None]).astype(jnp.bfloat16)
    dcontext = jnp.dot(grad_rows, w_out.T, preferred_element_type=jnp.float32).astype(jnp.bfloat16)

    qd = jnp.stack([qkv_local[:, 0], dcontext.reshape(tok_rows, H, head_size)], axis=1)
    qd_send = (
        qd.reshape(groups, part_rows, 2, H, head_size)
        .transpose(3, 0, 1, 2, 4)
        .reshape(seq_count, part_rows, 2, head_size)
    )
    paired = qkv_local[:, 1:].transpose(2, 0, 1, 3)
    paired_send = jnp.broadcast_to(paired[:, None], (H, groups, tok_rows, 2, head_size))
    paired_send = paired_send.reshape(seq_count, tok_rows, 2, head_size)
    qd_recv = lax.all_to_all(qd_send, "seq", split_axis=0, concat_axis=0, tiled=True)
    paired_recv = lax.all_to_all(paired_send, "seq", split_axis=0, concat_axis=0, tiled=True)
    queries = qd_recv[:, :, 0].reshape(seq_count * part_rows, head_size)
    dcontext_heads = qd_recv[:, :, 1].reshape(seq_count * part_rows, head_size)
    keys = paired_recv[:, :, 0].reshape(frame_total, head_size)
    values = paired_recv[:, :, 1].reshape(frame_total, head_size)
    position = jnp.arange(frame_total, dtype=jnp.int32)
    bias = jnp.where(position < length, 0.0, -1000000000.0).astype(jnp.float32)

    context_h, dquery, dkeys, dvalues = attn_pass(queries, keys, values, dcontext_heads, bias, scale)

    context_back = lax.all_to_all(
        context_h.reshape(seq_count, part_rows, head_size), "seq", split_axis=0, concat_axis=0, tiled=True
    )
    context = (
        context_back.reshape(H, groups, part_rows, head_size).transpose(1, 2, 0, 3).reshape(tok_rows, width)
    )
    branch = jnp.dot(context, w_out, preferred_element_type=jnp.float32)
    output = (inputs + valid[:, None] * branch).astype(jnp.bfloat16)
    out_share = lax.psum_scatter(
        jnp.dot(context.T, grad_rows, preferred_element_type=jnp.float32),
        "seq",
        scatter_dimension=0,
        tiled=True,
    )

    split_grads = jnp.stack([dkeys, dvalues], axis=1).reshape(seq_count, groups, part_rows, 2, head_size)
    own_half = lax.dynamic_index_in_dim(split_grads, group_index, 1, keepdims=False)
    other_half = lax.dynamic_index_in_dim(split_grads, 1 - group_index, 1, keepdims=False)
    partner_half = from_partner(other_half, "seq", 0)
    paired_rows = (own_half + partner_half).astype(jnp.bfloat16)
    dtrio = jnp.concatenate([dquery.reshape(seq_count, part_rows, 1, head_size), paired_rows], axis=2)
    returned_grads = lax.all_to_all(dtrio, "seq", split_axis=0, concat_axis=0, tiled=True)
    dqkv = returned_grads.reshape(H, groups, part_rows, 3, head_size)
    dqkv = dqkv.transpose(1, 2, 3, 0, 4).reshape(tok_rows, 3 * width)
    qkv_share = lax.psum_scatter(
        jnp.dot(normed.T, dqkv, preferred_element_type=jnp.float32),
        "seq",
        scatter_dimension=0,
        tiled=True,
    )
    grad_qkv, grad_out = lax.psum((qkv_share, out_share), "batch")
    dnormed = jnp.dot(dqkv, w_qkv.T, preferred_element_type=jnp.float32)
    unused, pull = jax.vjp(layer_norm, inputs)
    grad_input = (cotangent[0].astype(jnp.float32) + pull(dnormed)[0]).astype(jnp.bfloat16)
    return (output[None], grad_input[None], grad_qkv, grad_out)


def solution(mesh):
    return jax.shard_map(
        per_device,
        mesh=mesh,
        in_specs=(P("batch", "seq", None), P("batch"), P(), P(), P("batch", "seq", None)),
        out_specs=(
            P("batch", "seq", None),
            P("batch", "seq", None),
            P("seq", None),
            P("seq", None),
        ),
        check_vma=False,
    )
```

```python
import jax
import jax.numpy as jnp
from jax import lax
from jax.sharding import PartitionSpec as P
from jax.experimental import pallas as pl
from jax.experimental.pallas import tpu as pltpu
import functools

H = 8


def from_partner(array, axis, stride):
    return lax.ppermute(array, axis, [(i, i ^ 1 << stride) for i in range(lax.axis_size(axis))])


def layer_norm(values):
    mean = jnp.mean(values, axis=-1, keepdims=True)
    centred = values - mean
    var = jnp.mean(centred * centred, axis=-1, keepdims=True)
    return centred * lax.rsqrt(var + 1e-05)


def _attn_kernel(q_ref, do_ref, k_ref, v_ref, bias_ref, ctx_ref, dq_ref, dk_ref, dv_ref, *, scale):
    i = pl.program_id(0)

    @pl.when(i == 0)
    def _():
        dk_ref[...] = jnp.zeros_like(dk_ref)
        dv_ref[...] = jnp.zeros_like(dv_ref)

    q = q_ref[...]
    do = do_ref[...]
    k = k_ref[...]
    v = v_ref[...]
    nt = (((1,), (1,)), ((), ()))
    tn = (((0,), (0,)), ((), ()))
    s = lax.dot_general(q, k, nt, preferred_element_type=jnp.float32) * scale + bias_ref[...]
    m = jnp.max(s, axis=1, keepdims=True)
    e = jnp.exp(s - m)
    p = e / jnp.sum(e, axis=1, keepdims=True)
    p16 = p.astype(jnp.bfloat16)
    ctx_ref[...] = jnp.dot(p16, v, preferred_element_type=jnp.float32).astype(ctx_ref.dtype)
    dp = lax.dot_general(do, v, nt, preferred_element_type=jnp.float32)
    delta = jnp.sum(p * dp, axis=1, keepdims=True)
    ds = (p * (dp - delta)).astype(jnp.bfloat16)
    dq_ref[...] = (jnp.dot(ds, k, preferred_element_type=jnp.float32) * scale).astype(dq_ref.dtype)
    dk_ref[...] += lax.dot_general(ds, q, tn, preferred_element_type=jnp.float32) * scale
    dv_ref[...] += lax.dot_general(p16, do, tn, preferred_element_type=jnp.float32)


def attn_pass(query, keys, values, dcontext, bias, scale, block=256, interpret=False):
    nq, hd = query.shape
    nk = keys.shape[0]
    grid = (nq // block,)
    kernel = functools.partial(_attn_kernel, scale=scale)
    return pl.pallas_call(
        kernel,
        grid=grid,
        in_specs=[
            pl.BlockSpec((block, hd), lambda i: (i, 0)),
            pl.BlockSpec((block, hd), lambda i: (i, 0)),
            pl.BlockSpec((nk, hd), lambda i: (0, 0)),
            pl.BlockSpec((nk, hd), lambda i: (0, 0)),
            pl.BlockSpec((1, nk), lambda i: (0, 0)),
        ],
        out_specs=[
            pl.BlockSpec((block, hd), lambda i: (i, 0)),
            pl.BlockSpec((block, hd), lambda i: (i, 0)),
            pl.BlockSpec((nk, hd), lambda i: (0, 0)),
            pl.BlockSpec((nk, hd), lambda i: (0, 0)),
        ],
        out_shape=[
            jax.ShapeDtypeStruct((nq, hd), jnp.bfloat16),
            jax.ShapeDtypeStruct((nq, hd), jnp.bfloat16),
            jax.ShapeDtypeStruct((nk, hd), jnp.float32),
            jax.ShapeDtypeStruct((nk, hd), jnp.float32),
        ],
        compiler_params=pltpu.CompilerParams(dimension_semantics=("arbitrary",)),
        interpret=interpret,
    )(query, dcontext, keys, values, bias.reshape(1, nk))


def per_device(frames, lengths, w_qkv, w_out, cotangent):
    width = w_out.shape[0]
    head_size = width // H
    scale = float(head_size) ** (-0.5)
    tok_rows = frames.shape[1]
    seq_count = lax.axis_size("seq")
    groups = seq_count // H
    part_rows = tok_rows // groups
    frame_total = tok_rows * seq_count
    group_index = lax.axis_index("seq") % groups
    length = lengths[0]
    inputs = frames[0].astype(jnp.float32)
    normed = layer_norm(inputs).astype(jnp.bfloat16)
    qkv = jnp.dot(normed, w_qkv, preferred_element_type=jnp.float32).astype(jnp.bfloat16)
    qkv_local = qkv.reshape(tok_rows, 3, H, head_size)
    offset = lax.axis_index("seq") * tok_rows
    own_pos = offset + jnp.arange(tok_rows, dtype=jnp.int32)
    valid = (own_pos < length).astype(jnp.float32)
    grad_rows = (cotangent[0].astype(jnp.float32) * valid[:, None]).astype(jnp.bfloat16)
    dcontext = jnp.dot(grad_rows, w_out.T, preferred_element_type=jnp.float32).astype(jnp.bfloat16)

    qd = jnp.stack([qkv_local[:, 0], dcontext.reshape(tok_rows, H, head_size)], axis=1)
    qd_send = (
        qd.reshape(groups, part_rows, 2, H, head_size)
        .transpose(3, 0, 1, 2, 4)
        .reshape(seq_count, part_rows * 2, head_size)
    )
    paired = qkv_local[:, 1:].transpose(2, 0, 1, 3)
    paired_send = jnp.broadcast_to(paired[:, None], (H, groups, tok_rows, 2, head_size))
    paired_send = paired_send.reshape(seq_count, tok_rows * 2, head_size)
    recv = lax.all_to_all(
        jnp.concatenate([qd_send, paired_send], axis=1), "seq", split_axis=0, concat_axis=0, tiled=True
    )
    qd_recv = recv[:, : part_rows * 2].reshape(seq_count, part_rows, 2, head_size)
    paired_recv = recv[:, part_rows * 2 :].reshape(seq_count, tok_rows, 2, head_size)
    queries = qd_recv[:, :, 0].reshape(seq_count * part_rows, head_size)
    dcontext_heads = qd_recv[:, :, 1].reshape(seq_count * part_rows, head_size)
    keys = paired_recv[:, :, 0].reshape(frame_total, head_size)
    values = paired_recv[:, :, 1].reshape(frame_total, head_size)
    position = jnp.arange(frame_total, dtype=jnp.int32)
    bias = jnp.where(position < length, 0.0, -1000000000.0).astype(jnp.float32)

    context_h, dquery, dkeys, dvalues = attn_pass(queries, keys, values, dcontext_heads, bias, scale)

    context_back = lax.all_to_all(
        context_h.reshape(seq_count, part_rows, head_size), "seq", split_axis=0, concat_axis=0, tiled=True
    )
    context = (
        context_back.reshape(H, groups, part_rows, head_size).transpose(1, 2, 0, 3).reshape(tok_rows, width)
    )
    branch = jnp.dot(context, w_out, preferred_element_type=jnp.float32)
    output = (inputs + valid[:, None] * branch).astype(jnp.bfloat16)
    out_share = lax.psum_scatter(
        jnp.dot(context.T, grad_rows, preferred_element_type=jnp.float32),
        "seq",
        scatter_dimension=0,
        tiled=True,
    )

    split_grads = jnp.stack([dkeys, dvalues], axis=1).reshape(seq_count, groups, part_rows, 2, head_size)
    own_half = lax.dynamic_index_in_dim(split_grads, group_index, 1, keepdims=False)
    other_half = lax.dynamic_index_in_dim(split_grads, 1 - group_index, 1, keepdims=False)
    partner_half = from_partner(other_half.astype(jnp.bfloat16), "seq", 0)
    paired_rows = (own_half + partner_half.astype(jnp.float32)).astype(jnp.bfloat16)
    dtrio = jnp.concatenate([dquery.reshape(seq_count, part_rows, 1, head_size), paired_rows], axis=2)
    returned_grads = lax.all_to_all(dtrio, "seq", split_axis=0, concat_axis=0, tiled=True)
    dqkv = returned_grads.reshape(H, groups, part_rows, 3, head_size)
    dqkv = dqkv.transpose(1, 2, 3, 0, 4).reshape(tok_rows, 3 * width)
    qkv_share = lax.psum_scatter(
        jnp.dot(normed.T, dqkv, preferred_element_type=jnp.float32).astype(jnp.bfloat16),
        "seq",
        scatter_dimension=0,
        tiled=True,
    ).astype(jnp.float32)
    batch_count = lax.axis_size("batch")
    shares = jnp.concatenate([qkv_share, out_share], axis=1)
    share_rows = shares.shape[0] // batch_count
    pieces = lax.all_to_all(
        shares.reshape(batch_count, share_rows, shares.shape[1]), "batch", split_axis=0, concat_axis=0, tiled=True
    )
    summed = lax.all_gather(jnp.sum(pieces, axis=0), "batch", axis=0, tiled=True)
    grad_qkv = summed[:, : qkv_share.shape[1]]
    grad_out = summed[:, qkv_share.shape[1] :]
    dnormed = jnp.dot(dqkv, w_qkv.T, preferred_element_type=jnp.float32)
    unused, pull = jax.vjp(layer_norm, inputs)
    grad_input = (cotangent[0].astype(jnp.float32) + pull(dnormed)[0]).astype(jnp.bfloat16)
    return (output[None], grad_input[None], grad_qkv, grad_out)


def solution(mesh):
    return jax.shard_map(
        per_device,
        mesh=mesh,
        in_specs=(P("batch", "seq", None), P("batch"), P(), P(), P("batch", "seq", None)),
        out_specs=(
            P("batch", "seq", None),
            P("batch", "seq", None),
            P("seq", None),
            P("seq", None),
        ),
        check_vma=False,
    )
```

```python
import jax
import jax.numpy as jnp
from jax import lax
from jax.sharding import PartitionSpec as P
from jax.experimental import pallas as pl
from jax.experimental.pallas import tpu as pltpu
import functools

H = 8


def from_partner(array, axis, stride):
    return lax.ppermute(array, axis, [(i, i ^ 1 << stride) for i in range(lax.axis_size(axis))])


def layer_norm(values):
    mean = jnp.mean(values, axis=-1, keepdims=True)
    centred = values - mean
    var = jnp.mean(centred * centred, axis=-1, keepdims=True)
    return centred * lax.rsqrt(var + 1e-05)


def _attn_kernel(q_ref, do_ref, k_ref, v_ref, bias_ref, ctx_ref, dq_ref, dk_ref, dv_ref, *, scale):
    i = pl.program_id(0)

    @pl.when(i == 0)
    def _():
        dk_ref[...] = jnp.zeros_like(dk_ref)
        dv_ref[...] = jnp.zeros_like(dv_ref)

    q = q_ref[...]
    do = do_ref[...]
    k = k_ref[...]
    v = v_ref[...]
    nt = (((1,), (1,)), ((), ()))
    tn = (((0,), (0,)), ((), ()))
    s = lax.dot_general(q, k, nt, preferred_element_type=jnp.float32) * scale + bias_ref[...]
    m = jnp.max(s, axis=1, keepdims=True)
    e = jnp.exp(s - m)
    p = e / jnp.sum(e, axis=1, keepdims=True)
    p16 = p.astype(jnp.bfloat16)
    ctx_ref[...] = jnp.dot(p16, v, preferred_element_type=jnp.float32).astype(ctx_ref.dtype)
    dp = lax.dot_general(do, v, nt, preferred_element_type=jnp.float32)
    delta = jnp.sum(p * dp, axis=1, keepdims=True)
    ds = (p * (dp - delta)).astype(jnp.bfloat16)
    dq_ref[...] = (jnp.dot(ds, k, preferred_element_type=jnp.float32) * scale).astype(dq_ref.dtype)
    dk_ref[...] += lax.dot_general(ds, q, tn, preferred_element_type=jnp.float32) * scale
    dv_ref[...] += lax.dot_general(p16, do, tn, preferred_element_type=jnp.float32)


def attn_pass(query, keys, values, dcontext, bias, scale, block=256, interpret=False):
    nq, hd = query.shape
    nk = keys.shape[0]
    grid = (nq // block,)
    kernel = functools.partial(_attn_kernel, scale=scale)
    return pl.pallas_call(
        kernel,
        grid=grid,
        in_specs=[
            pl.BlockSpec((block, hd), lambda i: (i, 0)),
            pl.BlockSpec((block, hd), lambda i: (i, 0)),
            pl.BlockSpec((nk, hd), lambda i: (0, 0)),
            pl.BlockSpec((nk, hd), lambda i: (0, 0)),
            pl.BlockSpec((1, nk), lambda i: (0, 0)),
        ],
        out_specs=[
            pl.BlockSpec((block, hd), lambda i: (i, 0)),
            pl.BlockSpec((block, hd), lambda i: (i, 0)),
            pl.BlockSpec((nk, hd), lambda i: (0, 0)),
            pl.BlockSpec((nk, hd), lambda i: (0, 0)),
        ],
        out_shape=[
            jax.ShapeDtypeStruct((nq, hd), jnp.bfloat16),
            jax.ShapeDtypeStruct((nq, hd), jnp.bfloat16),
            jax.ShapeDtypeStruct((nk, hd), jnp.float32),
            jax.ShapeDtypeStruct((nk, hd), jnp.float32),
        ],
        compiler_params=pltpu.CompilerParams(dimension_semantics=("arbitrary",)),
        interpret=interpret,
    )(query, dcontext, keys, values, bias.reshape(1, nk))


def per_device(frames, lengths, w_qkv, w_out, cotangent):
    width = w_out.shape[0]
    head_size = width // H
    scale = float(head_size) ** (-0.5)
    tok_rows = frames.shape[1]
    seq_count = lax.axis_size("seq")
    groups = seq_count // H
    part_rows = tok_rows // groups
    frame_total = tok_rows * seq_count
    group_index = lax.axis_index("seq") % groups
    length = lengths[0]
    inputs = frames[0].astype(jnp.float32)
    normed = layer_norm(inputs).astype(jnp.bfloat16)
    qkv = jnp.dot(normed, w_qkv, preferred_element_type=jnp.float32).astype(jnp.bfloat16)
    qkv_local = qkv.reshape(tok_rows, 3, H, head_size)
    offset = lax.axis_index("seq") * tok_rows
    own_pos = offset + jnp.arange(tok_rows, dtype=jnp.int32)
    valid = (own_pos < length).astype(jnp.float32)
    grad_rows = (cotangent[0].astype(jnp.float32) * valid[:, None]).astype(jnp.bfloat16)
    dcontext = jnp.dot(grad_rows, w_out.T, preferred_element_type=jnp.float32).astype(jnp.bfloat16)

    qd = jnp.stack([qkv_local[:, 0], dcontext.reshape(tok_rows, H, head_size)], axis=1)
    qd_send = (
        qd.reshape(groups, part_rows, 2, H, head_size)
        .transpose(3, 0, 1, 2, 4)
        .reshape(seq_count, part_rows * 2, head_size)
    )
    paired = qkv_local[:, 1:].transpose(2, 0, 1, 3)
    paired_send = jnp.broadcast_to(paired[:, None], (H, groups, tok_rows, 2, head_size))
    paired_send = paired_send.reshape(seq_count, tok_rows * 2, head_size)
    recv = lax.all_to_all(
        jnp.concatenate([qd_send, paired_send], axis=1), "seq", split_axis=0, concat_axis=0, tiled=True
    )
    qd_recv = recv[:, : part_rows * 2].reshape(seq_count, part_rows, 2, head_size)
    paired_recv = recv[:, part_rows * 2 :].reshape(seq_count, tok_rows, 2, head_size)
    queries = qd_recv[:, :, 0].reshape(seq_count * part_rows, head_size)
    dcontext_heads = qd_recv[:, :, 1].reshape(seq_count * part_rows, head_size)
    keys = paired_recv[:, :, 0].reshape(frame_total, head_size)
    values = paired_recv[:, :, 1].reshape(frame_total, head_size)
    position = jnp.arange(frame_total, dtype=jnp.int32)
    bias = jnp.where(position < length, 0.0, -1000000000.0).astype(jnp.float32)

    context_h, dquery, dkeys, dvalues = attn_pass(queries, keys, values, dcontext_heads, bias, scale)

    split_grads = jnp.stack([dkeys, dvalues], axis=1).reshape(seq_count, groups, part_rows, 2, head_size)
    own_half = lax.dynamic_index_in_dim(split_grads, group_index, 1, keepdims=False)
    other_half = lax.dynamic_index_in_dim(split_grads, 1 - group_index, 1, keepdims=False)
    partner_half = from_partner(other_half.astype(jnp.bfloat16), "seq", 0)
    paired_rows = (own_half + partner_half.astype(jnp.float32)).astype(jnp.bfloat16)
    back = jnp.concatenate(
        [
            context_h.reshape(seq_count, part_rows, 1, head_size),
            dquery.reshape(seq_count, part_rows, 1, head_size),
            paired_rows,
        ],
        axis=2,
    )
    returned = lax.all_to_all(back, "seq", split_axis=0, concat_axis=0, tiled=True)
    returned = returned.reshape(H, groups, part_rows, 4, head_size).transpose(1, 2, 3, 0, 4)
    context = returned[:, :, 0].reshape(tok_rows, width)
    dqkv = returned[:, :, 1:].reshape(tok_rows, 3 * width)
    branch = jnp.dot(context, w_out, preferred_element_type=jnp.float32)
    output = (inputs + valid[:, None] * branch).astype(jnp.bfloat16)
    partials = jnp.concatenate(
        [
            jnp.dot(normed.T, dqkv, preferred_element_type=jnp.float32),
            jnp.dot(context.T, grad_rows, preferred_element_type=jnp.float32),
        ],
        axis=1,
    )
    shares = lax.psum_scatter(
        partials.astype(jnp.bfloat16), "seq", scatter_dimension=0, tiled=True
    ).astype(jnp.float32)
    batch_count = lax.axis_size("batch")
    share_rows = shares.shape[0] // batch_count
    pieces = lax.all_to_all(
        shares.reshape(batch_count, share_rows, shares.shape[1]), "batch", split_axis=0, concat_axis=0, tiled=True
    )
    summed = lax.all_gather(jnp.sum(pieces, axis=0), "batch", axis=0, tiled=True)
    grad_qkv = summed[:, : 3 * width]
    grad_out = summed[:, 3 * width :]
    dnormed = jnp.dot(dqkv, w_qkv.T, preferred_element_type=jnp.float32)
    unused, pull = jax.vjp(layer_norm, inputs)
    grad_input = (cotangent[0].astype(jnp.float32) + pull(dnormed)[0]).astype(jnp.bfloat16)
    return (output[None], grad_input[None], grad_qkv, grad_out)


def solution(mesh):
    return jax.shard_map(
        per_device,
        mesh=mesh,
        in_specs=(P("batch", "seq", None), P("batch"), P(), P(), P("batch", "seq", None)),
        out_specs=(
            P("batch", "seq", None),
            P("batch", "seq", None),
            P("seq", None),
            P("seq", None),
        ),
        check_vma=False,
    )
```

```python
import jax
import jax.numpy as jnp
from jax import lax
from jax.sharding import PartitionSpec as P
from jax.experimental import pallas as pl
from jax.experimental.pallas import tpu as pltpu
import functools

H = 8


def from_partner(array, axis, stride):
    return lax.ppermute(array, axis, [(i, i ^ 1 << stride) for i in range(lax.axis_size(axis))])


def layer_norm(values):
    mean = jnp.mean(values, axis=-1, keepdims=True)
    centred = values - mean
    var = jnp.mean(centred * centred, axis=-1, keepdims=True)
    return centred * lax.rsqrt(var + 1e-05)


def _attn_kernel(q_ref, do_ref, k_ref, v_ref, bias_ref, ctx_ref, dq_ref, dk_ref, dv_ref, *, scale):
    i = pl.program_id(0)

    @pl.when(i == 0)
    def _():
        dk_ref[...] = jnp.zeros_like(dk_ref)
        dv_ref[...] = jnp.zeros_like(dv_ref)

    q = q_ref[...]
    do = do_ref[...]
    k = k_ref[...]
    v = v_ref[...]
    nt = (((1,), (1,)), ((), ()))
    tn = (((0,), (0,)), ((), ()))
    s = lax.dot_general(q, k, nt, preferred_element_type=jnp.float32) * scale + bias_ref[...]
    m = jnp.max(s, axis=1, keepdims=True)
    e = jnp.exp(s - m)
    p = e / jnp.sum(e, axis=1, keepdims=True)
    p16 = p.astype(jnp.bfloat16)
    ctx_ref[...] = jnp.dot(p16, v, preferred_element_type=jnp.float32).astype(ctx_ref.dtype)
    dp = lax.dot_general(do, v, nt, preferred_element_type=jnp.float32)
    delta = jnp.sum(p * dp, axis=1, keepdims=True)
    ds = (p * (dp - delta)).astype(jnp.bfloat16)
    dq_ref[...] = (jnp.dot(ds, k, preferred_element_type=jnp.float32) * scale).astype(dq_ref.dtype)
    dk_ref[...] += lax.dot_general(ds, q, tn, preferred_element_type=jnp.float32) * scale
    dv_ref[...] += lax.dot_general(p16, do, tn, preferred_element_type=jnp.float32)


def attn_pass(query, keys, values, dcontext, bias, scale, block=256, interpret=False):
    nq, hd = query.shape
    nk = keys.shape[0]
    grid = (nq // block,)
    kernel = functools.partial(_attn_kernel, scale=scale)
    return pl.pallas_call(
        kernel,
        grid=grid,
        in_specs=[
            pl.BlockSpec((block, hd), lambda i: (i, 0)),
            pl.BlockSpec((block, hd), lambda i: (i, 0)),
            pl.BlockSpec((nk, hd), lambda i: (0, 0)),
            pl.BlockSpec((nk, hd), lambda i: (0, 0)),
            pl.BlockSpec((1, nk), lambda i: (0, 0)),
        ],
        out_specs=[
            pl.BlockSpec((block, hd), lambda i: (i, 0)),
            pl.BlockSpec((block, hd), lambda i: (i, 0)),
            pl.BlockSpec((nk, hd), lambda i: (0, 0)),
            pl.BlockSpec((nk, hd), lambda i: (0, 0)),
        ],
        out_shape=[
            jax.ShapeDtypeStruct((nq, hd), jnp.bfloat16),
            jax.ShapeDtypeStruct((nq, hd), jnp.bfloat16),
            jax.ShapeDtypeStruct((nk, hd), jnp.float32),
            jax.ShapeDtypeStruct((nk, hd), jnp.float32),
        ],
        compiler_params=pltpu.CompilerParams(dimension_semantics=("arbitrary",)),
        interpret=interpret,
    )(query, dcontext, keys, values, bias.reshape(1, nk))


def per_device(frames, lengths, w_qkv, w_out, cotangent):
    width = w_out.shape[0]
    head_size = width // H
    scale = float(head_size) ** (-0.5)
    tok_rows = frames.shape[1]
    seq_count = lax.axis_size("seq")
    groups = seq_count // H
    part_rows = tok_rows // groups
    frame_total = tok_rows * seq_count
    group_index = lax.axis_index("seq") % groups
    length = lengths[0]
    inputs = frames[0].astype(jnp.float32)
    normed = layer_norm(inputs).astype(jnp.bfloat16)
    qkv = jnp.dot(normed, w_qkv, preferred_element_type=jnp.float32).astype(jnp.bfloat16)
    qkv_local = qkv.reshape(tok_rows, 3, H, head_size)
    offset = lax.axis_index("seq") * tok_rows
    own_pos = offset + jnp.arange(tok_rows, dtype=jnp.int32)
    valid = (own_pos < length).astype(jnp.float32)
    grad_rows = (cotangent[0].astype(jnp.float32) * valid[:, None]).astype(jnp.bfloat16)
    dcontext = jnp.dot(grad_rows, w_out.T, preferred_element_type=jnp.float32).astype(jnp.bfloat16)

    qd = jnp.stack([qkv_local[:, 0], dcontext.reshape(tok_rows, H, head_size)], axis=1)
    qd_send = (
        qd.reshape(groups, part_rows, 2, H, head_size)
        .transpose(3, 0, 1, 2, 4)
        .reshape(seq_count, part_rows * 2, head_size)
    )
    paired = qkv_local[:, 1:].transpose(2, 0, 1, 3)
    paired_send = jnp.broadcast_to(paired[:, None], (H, groups, tok_rows, 2, head_size))
    paired_send = paired_send.reshape(seq_count, tok_rows * 2, head_size)
    recv = lax.all_to_all(
        jnp.concatenate([qd_send, paired_send], axis=1), "seq", split_axis=0, concat_axis=0, tiled=True
    )
    normed_send = jnp.broadcast_to(normed.reshape(1, groups, part_rows, width), (H, groups, part_rows, width))
    normed_recv = lax.all_to_all(
        normed_send.reshape(seq_count, part_rows, width), "seq", split_axis=0, concat_axis=0, tiled=True
    ).reshape(seq_count * part_rows, width)
    qd_recv = recv[:, : part_rows * 2].reshape(seq_count, part_rows, 2, head_size)
    paired_recv = recv[:, part_rows * 2 :].reshape(seq_count, tok_rows, 2, head_size)
    queries = qd_recv[:, :, 0].reshape(seq_count * part_rows, head_size)
    dcontext_heads = qd_recv[:, :, 1].reshape(seq_count * part_rows, head_size)
    keys = paired_recv[:, :, 0].reshape(frame_total, head_size)
    values = paired_recv[:, :, 1].reshape(frame_total, head_size)
    position = jnp.arange(frame_total, dtype=jnp.int32)
    bias = jnp.where(position < length, 0.0, -1000000000.0).astype(jnp.float32)

    context_h, dquery, dkeys, dvalues = attn_pass(queries, keys, values, dcontext_heads, bias, scale)

    split_grads = jnp.stack([dkeys, dvalues], axis=1).reshape(seq_count, groups, part_rows, 2, head_size)
    own_half = lax.dynamic_index_in_dim(split_grads, group_index, 1, keepdims=False)
    other_half = lax.dynamic_index_in_dim(split_grads, 1 - group_index, 1, keepdims=False)
    partner_half = from_partner(other_half.astype(jnp.bfloat16), "seq", 0)
    paired_rows = (own_half + partner_half.astype(jnp.float32)).astype(jnp.bfloat16)
    back = jnp.concatenate(
        [
            context_h.reshape(seq_count, part_rows, 1, head_size),
            dquery.reshape(seq_count, part_rows, 1, head_size),
            paired_rows,
        ],
        axis=2,
    )
    returned = lax.all_to_all(back, "seq", split_axis=0, concat_axis=0, tiled=True)
    returned = returned.reshape(H, groups, part_rows, 4, head_size).transpose(1, 2, 3, 0, 4)
    context = returned[:, :, 0].reshape(tok_rows, width)
    dqkv = returned[:, :, 1:].reshape(tok_rows, 3 * width)
    branch = jnp.dot(context, w_out, preferred_element_type=jnp.float32)
    output = (inputs + valid[:, None] * branch).astype(jnp.bfloat16)
    dqkv_head = jnp.concatenate([dquery.reshape(seq_count, part_rows, 1, head_size), paired_rows], axis=2)
    qkv_part = jnp.dot(
        normed_recv.T, dqkv_head.reshape(seq_count * part_rows, 3 * head_size), preferred_element_type=jnp.float32
    )
    out_part = jnp.dot(context.T, grad_rows, preferred_element_type=jnp.float32)
    share_rows = width // seq_count
    parts = jnp.concatenate([qkv_part, out_part], axis=1).astype(jnp.bfloat16)
    gathered = lax.all_to_all(
        parts.reshape(seq_count, share_rows, parts.shape[1]), "seq", split_axis=0, concat_axis=0, tiled=True
    ).astype(jnp.float32)
    qkv_rows = (
        jnp.sum(gathered[:, :, : 3 * head_size].reshape(H, groups, share_rows, 3, head_size), axis=1)
        .transpose(1, 2, 0, 3)
        .reshape(share_rows, 3 * width)
    )
    out_rows = jnp.sum(gathered[:, :, 3 * head_size :], axis=0)
    shares = jnp.concatenate([qkv_rows, out_rows], axis=1)
    batch_count = lax.axis_size("batch")
    share_rows = shares.shape[0] // batch_count
    pieces = lax.all_to_all(
        shares.reshape(batch_count, share_rows, shares.shape[1]), "batch", split_axis=0, concat_axis=0, tiled=True
    )
    summed = lax.all_gather(jnp.sum(pieces, axis=0), "batch", axis=0, tiled=True)
    grad_qkv = summed[:, : 3 * width]
    grad_out = summed[:, 3 * width :]
    dnormed = jnp.dot(dqkv, w_qkv.T, preferred_element_type=jnp.float32)
    unused, pull = jax.vjp(layer_norm, inputs)
    grad_input = (cotangent[0].astype(jnp.float32) + pull(dnormed)[0]).astype(jnp.bfloat16)
    return (output[None], grad_input[None], grad_qkv, grad_out)


def solution(mesh):
    return jax.shard_map(
        per_device,
        mesh=mesh,
        in_specs=(P("batch", "seq", None), P("batch"), P(), P(), P("batch", "seq", None)),
        out_specs=(
            P("batch", "seq", None),
            P("batch", "seq", None),
            P("seq", None),
            P("seq", None),
        ),
        check_vma=False,
    )
```

```python
import jax
import jax.numpy as jnp
from jax import lax
from jax.sharding import PartitionSpec as P
from jax.experimental import pallas as pl
from jax.experimental.pallas import tpu as pltpu
import functools

H = 8


def from_partner(array, axis, stride):
    return lax.ppermute(array, axis, [(i, i ^ 1 << stride) for i in range(lax.axis_size(axis))])


def layer_norm(values):
    mean = jnp.mean(values, axis=-1, keepdims=True)
    centred = values - mean
    var = jnp.mean(centred * centred, axis=-1, keepdims=True)
    return centred * lax.rsqrt(var + 1e-05)


def _attn_kernel(q_ref, do_ref, k_ref, v_ref, bias_ref, ctx_ref, dq_ref, dk_ref, dv_ref, *, scale):
    i = pl.program_id(0)

    @pl.when(i == 0)
    def _():
        dk_ref[...] = jnp.zeros_like(dk_ref)
        dv_ref[...] = jnp.zeros_like(dv_ref)

    nb, rows, hd = q_ref.shape
    ns, kr, _ = k_ref.shape
    q = q_ref[...].reshape(nb * rows, hd)
    do = do_ref[...].reshape(nb * rows, hd)
    k = k_ref[...].reshape(ns * kr, hd)
    v = v_ref[...].reshape(ns * kr, hd)
    nt = (((1,), (1,)), ((), ()))
    tn = (((0,), (0,)), ((), ()))
    s = lax.dot_general(q, k, nt, preferred_element_type=jnp.float32) * scale + bias_ref[...]
    m = jnp.max(s, axis=1, keepdims=True)
    e = jnp.exp(s - m)
    p = e / jnp.sum(e, axis=1, keepdims=True)
    p16 = p.astype(jnp.bfloat16)
    ctx = jnp.dot(p16, v, preferred_element_type=jnp.float32)
    ctx_ref[...] = ctx.reshape(nb, rows, hd).astype(ctx_ref.dtype)
    dp = lax.dot_general(do, v, nt, preferred_element_type=jnp.float32)
    delta = jnp.sum(p * dp, axis=1, keepdims=True)
    ds = (p * (dp - delta)).astype(jnp.bfloat16)
    dq = jnp.dot(ds, k, preferred_element_type=jnp.float32) * scale
    dq_ref[...] = dq.reshape(nb, rows, hd).astype(dq_ref.dtype)
    dk_ref[...] += lax.dot_general(ds, q, tn, preferred_element_type=jnp.float32) * scale
    dv_ref[...] += lax.dot_general(p16, do, tn, preferred_element_type=jnp.float32)


def attn_pass(recv, part_rows, bias, scale, block_sources=2):
    sources, _, hd = recv.shape
    key_rows = 2 * part_rows
    nq = sources * part_rows
    nk = sources * key_rows
    kernel = functools.partial(_attn_kernel, scale=scale)
    return pl.pallas_call(
        kernel,
        grid=(sources // block_sources,),
        in_specs=[
            pl.BlockSpec((block_sources, part_rows, hd), lambda i: (i, 0, 0)),
            pl.BlockSpec((block_sources, part_rows, hd), lambda i: (i, 1, 0)),
            pl.BlockSpec((sources, key_rows, hd), lambda i: (0, 1, 0)),
            pl.BlockSpec((sources, key_rows, hd), lambda i: (0, 2, 0)),
            pl.BlockSpec((1, nk), lambda i: (0, 0)),
        ],
        out_specs=[
            pl.BlockSpec((block_sources, part_rows, hd), lambda i: (i, 0, 0)),
            pl.BlockSpec((block_sources, part_rows, hd), lambda i: (i, 0, 0)),
            pl.BlockSpec((nk, hd), lambda i: (0, 0)),
            pl.BlockSpec((nk, hd), lambda i: (0, 0)),
        ],
        out_shape=[
            jax.ShapeDtypeStruct((sources, part_rows, hd), jnp.bfloat16),
            jax.ShapeDtypeStruct((sources, part_rows, hd), jnp.bfloat16),
            jax.ShapeDtypeStruct((nk, hd), jnp.float32),
            jax.ShapeDtypeStruct((nk, hd), jnp.float32),
        ],
        compiler_params=pltpu.CompilerParams(dimension_semantics=("arbitrary",)),
    )(recv, recv, recv, recv, bias.reshape(1, nk))


def per_device(frames, lengths, w_qkv, w_out, cotangent):
    width = w_out.shape[0]
    head_size = width // H
    scale = float(head_size) ** (-0.5)
    tok_rows = frames.shape[1]
    seq_count = lax.axis_size("seq")
    groups = seq_count // H
    part_rows = tok_rows // groups
    frame_total = tok_rows * seq_count
    group_index = lax.axis_index("seq") % groups
    length = lengths[0]
    inputs = frames[0].astype(jnp.float32)
    normed = layer_norm(inputs).astype(jnp.bfloat16)
    qkv = jnp.dot(normed, w_qkv, preferred_element_type=jnp.float32).astype(jnp.bfloat16)
    qkv_local = qkv.reshape(tok_rows, 3, H, head_size)
    offset = lax.axis_index("seq") * tok_rows
    own_pos = offset + jnp.arange(tok_rows, dtype=jnp.int32)
    valid = (own_pos < length).astype(jnp.float32)
    grad_rows = (cotangent[0].astype(jnp.float32) * valid[:, None]).astype(jnp.bfloat16)
    dcontext = jnp.dot(grad_rows, w_out.T, preferred_element_type=jnp.float32).astype(jnp.bfloat16)

    def by_half(rows_heads):
        return rows_heads.reshape(groups, part_rows, H, head_size).transpose(2, 0, 1, 3).reshape(
            seq_count, part_rows, head_size
        )

    def to_both(rows_heads):
        both = jnp.broadcast_to(rows_heads.transpose(1, 0, 2)[:, None], (H, groups, tok_rows, head_size))
        return both.reshape(seq_count, tok_rows, head_size)

    send = jnp.concatenate(
        [
            by_half(qkv_local[:, 0]),
            by_half(dcontext.reshape(tok_rows, H, head_size)),
            to_both(qkv_local[:, 1]),
            to_both(qkv_local[:, 2]),
        ],
        axis=1,
    )
    recv = lax.all_to_all(send, "seq", split_axis=0, concat_axis=0, tiled=True)
    normed_send = jnp.broadcast_to(normed.reshape(1, groups, part_rows, width), (H, groups, part_rows, width))
    normed_recv = lax.all_to_all(
        normed_send.reshape(seq_count, part_rows, width), "seq", split_axis=0, concat_axis=0, tiled=True
    )
    position = jnp.arange(frame_total, dtype=jnp.int32)
    bias = jnp.where(position < length, 0.0, -1000000000.0).astype(jnp.float32)

    context_h, dquery, dkeys, dvalues = attn_pass(recv, part_rows, bias, scale)

    split_grads = jnp.stack([dkeys, dvalues], axis=1).reshape(seq_count, groups, part_rows, 2, head_size)
    own_half = lax.dynamic_index_in_dim(split_grads, group_index, 1, keepdims=False)
    other_half = lax.dynamic_index_in_dim(split_grads, 1 - group_index, 1, keepdims=False)
    partner_half = from_partner(other_half.astype(jnp.bfloat16), "seq", 0)
    paired_rows = (own_half + partner_half.astype(jnp.float32)).astype(jnp.bfloat16)
    back = jnp.concatenate(
        [
            context_h.reshape(seq_count, part_rows, 1, head_size),
            dquery.reshape(seq_count, part_rows, 1, head_size),
            paired_rows,
        ],
        axis=2,
    )
    returned = lax.all_to_all(back, "seq", split_axis=0, concat_axis=0, tiled=True)
    returned = returned.reshape(H, groups, part_rows, 4, head_size).transpose(1, 2, 3, 0, 4)
    context = returned[:, :, 0].reshape(tok_rows, width)
    dqkv = returned[:, :, 1:].reshape(tok_rows, 3 * width)
    branch = jnp.dot(context, w_out, preferred_element_type=jnp.float32)
    output = (inputs + valid[:, None] * branch).astype(jnp.bfloat16)
    over_frames = (((0, 1), (0, 1)), ((), ()))
    qkv_part = jnp.stack(
        [
            lax.dot_general(normed_recv, piece, over_frames, preferred_element_type=jnp.float32)
            for piece in (dquery, paired_rows[:, :, 0], paired_rows[:, :, 1])
        ],
        axis=1,
    ).reshape(width, 3 * head_size)
    out_part = jnp.dot(context.T, grad_rows, preferred_element_type=jnp.float32)
    share_rows = width // seq_count
    parts = jnp.concatenate([qkv_part, out_part], axis=1).astype(jnp.bfloat16)
    gathered = lax.all_to_all(
        parts.reshape(seq_count, share_rows, parts.shape[1]), "seq", split_axis=0, concat_axis=0, tiled=True
    )
    qkv_rows = (
        jnp.sum(gathered[:, :, : 3 * head_size].astype(jnp.float32).reshape(H, groups, share_rows, 3 * head_size), axis=1)
        .reshape(H, share_rows, 3, head_size)
        .transpose(1, 2, 0, 3)
        .reshape(share_rows, 3 * width)
    )
    out_rows = jnp.sum(gathered[:, :, 3 * head_size :].astype(jnp.float32), axis=0)
    batch_count = lax.axis_size("batch")
    piece_rows = share_rows // batch_count
    shares = jnp.concatenate([qkv_rows, out_rows], axis=1).astype(jnp.bfloat16)
    pieces = lax.all_to_all(
        shares.reshape(batch_count, piece_rows, shares.shape[1]), "batch", split_axis=0, concat_axis=0, tiled=True
    )
    summed = jnp.sum(pieces.astype(jnp.float32), axis=0)
    grad_qkv, grad_out = lax.all_gather(
        (summed[:, : 3 * width], summed[:, 3 * width :]), "batch", axis=0, tiled=True
    )
    dnormed = jnp.dot(dqkv, w_qkv.T, preferred_element_type=jnp.float32)
    unused, pull = jax.vjp(layer_norm, inputs)
    grad_input = (cotangent[0].astype(jnp.float32) + pull(dnormed)[0]).astype(jnp.bfloat16)
    return (output[None], grad_input[None], grad_qkv, grad_out)


def solution(mesh):
    return jax.shard_map(
        per_device,
        mesh=mesh,
        in_specs=(P("batch", "seq", None), P("batch"), P(), P(), P("batch", "seq", None)),
        out_specs=(
            P("batch", "seq", None),
            P("batch", "seq", None),
            P("seq", None),
            P("seq", None),
        ),
        check_vma=False,
    )
```

```python
import jax
import jax.numpy as jnp
from jax import lax
from jax.sharding import PartitionSpec as P
from jax.experimental import pallas as pl
from jax.experimental.pallas import tpu as pltpu
import functools

H = 8


def from_partner(array, axis, stride):
    return lax.ppermute(array, axis, [(i, i ^ 1 << stride) for i in range(lax.axis_size(axis))])


def layer_norm(values):
    mean = jnp.mean(values, axis=-1, keepdims=True)
    centred = values - mean
    var = jnp.mean(centred * centred, axis=-1, keepdims=True)
    return centred * lax.rsqrt(var + 1e-05)


def _attn_kernel(q_ref, do_ref, k_ref, v_ref, bias_ref, ctx_ref, dq_ref, dk_ref, dv_ref, *, scale):
    i = pl.program_id(0)

    @pl.when(i == 0)
    def _():
        dk_ref[...] = jnp.zeros_like(dk_ref)
        dv_ref[...] = jnp.zeros_like(dv_ref)

    nb, rows, hd = q_ref.shape
    ns, kr, _ = k_ref.shape
    q = q_ref[...].reshape(nb * rows, hd)
    do = do_ref[...].reshape(nb * rows, hd)
    k = k_ref[...].reshape(ns * kr, hd)
    v = v_ref[...].reshape(ns * kr, hd)
    nt = (((1,), (1,)), ((), ()))
    tn = (((0,), (0,)), ((), ()))
    s = lax.dot_general(q, k, nt, preferred_element_type=jnp.float32) * scale + bias_ref[...]
    m = jnp.max(s, axis=1, keepdims=True)
    e = jnp.exp(s - m)
    p = e / jnp.sum(e, axis=1, keepdims=True)
    p16 = p.astype(jnp.bfloat16)
    ctx = jnp.dot(p16, v, preferred_element_type=jnp.float32)
    ctx_ref[...] = ctx.reshape(nb, rows, hd).astype(ctx_ref.dtype)
    dp = lax.dot_general(do, v, nt, preferred_element_type=jnp.float32)
    delta = jnp.sum(p * dp, axis=1, keepdims=True)
    ds = (p * (dp - delta)).astype(jnp.bfloat16)
    dq = jnp.dot(ds, k, preferred_element_type=jnp.float32) * scale
    dq_ref[...] = dq.reshape(nb, rows, hd).astype(dq_ref.dtype)
    dk_ref[...] += lax.dot_general(ds, q, tn, preferred_element_type=jnp.float32) * scale
    dv_ref[...] += lax.dot_general(p16, do, tn, preferred_element_type=jnp.float32)


def attn_pass(recv, part_rows, bias, scale, block_sources=4):
    sources, _, hd = recv.shape
    key_rows = 2 * part_rows
    nq = sources * part_rows
    nk = sources * key_rows
    kernel = functools.partial(_attn_kernel, scale=scale)
    return pl.pallas_call(
        kernel,
        grid=(sources // block_sources,),
        in_specs=[
            pl.BlockSpec((block_sources, part_rows, hd), lambda i: (i, 0, 0)),
            pl.BlockSpec((block_sources, part_rows, hd), lambda i: (i, 1, 0)),
            pl.BlockSpec((sources, key_rows, hd), lambda i: (0, 1, 0)),
            pl.BlockSpec((sources, key_rows, hd), lambda i: (0, 2, 0)),
            pl.BlockSpec((1, nk), lambda i: (0, 0)),
        ],
        out_specs=[
            pl.BlockSpec((block_sources, part_rows, hd), lambda i: (i, 0, 0)),
            pl.BlockSpec((block_sources, part_rows, hd), lambda i: (i, 0, 0)),
            pl.BlockSpec((nk, hd), lambda i: (0, 0)),
            pl.BlockSpec((nk, hd), lambda i: (0, 0)),
        ],
        out_shape=[
            jax.ShapeDtypeStruct((sources, part_rows, hd), jnp.bfloat16),
            jax.ShapeDtypeStruct((sources, part_rows, hd), jnp.bfloat16),
            jax.ShapeDtypeStruct((nk, hd), jnp.float32),
            jax.ShapeDtypeStruct((nk, hd), jnp.float32),
        ],
        compiler_params=pltpu.CompilerParams(dimension_semantics=("arbitrary",)),
    )(recv, recv, recv, recv, bias.reshape(1, nk))


def per_device(frames, lengths, w_qkv, w_out, cotangent):
    width = w_out.shape[0]
    head_size = width // H
    scale = float(head_size) ** (-0.5)
    tok_rows = frames.shape[1]
    seq_count = lax.axis_size("seq")
    groups = seq_count // H
    part_rows = tok_rows // groups
    frame_total = tok_rows * seq_count
    group_index = lax.axis_index("seq") % groups
    length = lengths[0]
    inputs = frames[0].astype(jnp.float32)
    normed = layer_norm(inputs).astype(jnp.bfloat16)
    qkv = jnp.dot(normed, w_qkv, preferred_element_type=jnp.float32).astype(jnp.bfloat16)
    qkv_local = qkv.reshape(tok_rows, 3, H, head_size)
    offset = lax.axis_index("seq") * tok_rows
    own_pos = offset + jnp.arange(tok_rows, dtype=jnp.int32)
    valid = (own_pos < length).astype(jnp.float32)
    grad_rows = (cotangent[0].astype(jnp.float32) * valid[:, None]).astype(jnp.bfloat16)
    dcontext = jnp.dot(grad_rows, w_out.T, preferred_element_type=jnp.float32).astype(jnp.bfloat16)

    def by_half(rows_heads):
        return rows_heads.reshape(groups, part_rows, H, head_size).transpose(2, 0, 1, 3).reshape(
            seq_count, part_rows, head_size
        )

    def to_both(rows_heads):
        both = jnp.broadcast_to(rows_heads.transpose(1, 0, 2)[:, None], (H, groups, tok_rows, head_size))
        return both.reshape(seq_count, tok_rows, head_size)

    send = jnp.concatenate(
        [
            by_half(qkv_local[:, 0]),
            by_half(dcontext.reshape(tok_rows, H, head_size)),
            to_both(qkv_local[:, 1]),
            to_both(qkv_local[:, 2]),
        ],
        axis=1,
    )
    recv = lax.all_to_all(send, "seq", split_axis=0, concat_axis=0, tiled=True)
    normed_send = jnp.broadcast_to(normed.reshape(1, groups, part_rows, width), (H, groups, part_rows, width))
    normed_recv = lax.all_to_all(
        normed_send.reshape(seq_count, part_rows, width), "seq", split_axis=0, concat_axis=0, tiled=True
    )
    position = jnp.arange(frame_total, dtype=jnp.int32)
    bias = jnp.where(position < length, 0.0, -1000000000.0).astype(jnp.float32)

    context_h, dquery, dkeys, dvalues = attn_pass(recv, part_rows, bias, scale)

    split_grads = jnp.stack([dkeys, dvalues], axis=1).reshape(seq_count, groups, part_rows, 2, head_size)
    own_half = lax.dynamic_index_in_dim(split_grads, group_index, 1, keepdims=False)
    other_half = lax.dynamic_index_in_dim(split_grads, 1 - group_index, 1, keepdims=False)
    partner_half = from_partner(other_half.astype(jnp.bfloat16), "seq", 0)
    paired_rows = (own_half + partner_half.astype(jnp.float32)).astype(jnp.bfloat16)
    back = jnp.concatenate(
        [
            context_h.reshape(seq_count, part_rows, 1, head_size),
            dquery.reshape(seq_count, part_rows, 1, head_size),
            paired_rows,
        ],
        axis=2,
    )
    returned = lax.all_to_all(back, "seq", split_axis=0, concat_axis=0, tiled=True)
    returned = returned.reshape(H, groups, part_rows, 4, head_size).transpose(1, 2, 3, 0, 4)
    context = returned[:, :, 0].reshape(tok_rows, width)
    dqkv = returned[:, :, 1:].reshape(tok_rows, 3 * width)
    branch = jnp.dot(context, w_out, preferred_element_type=jnp.float32)
    output = (inputs + valid[:, None] * branch).astype(jnp.bfloat16)
    over_frames = (((0, 1), (0, 1)), ((), ()))
    qkv_part = jnp.stack(
        [
            lax.dot_general(normed_recv, piece, over_frames, preferred_element_type=jnp.float32)
            for piece in (dquery, paired_rows[:, :, 0], paired_rows[:, :, 1])
        ],
        axis=1,
    ).reshape(width, 3 * head_size)
    out_part = jnp.dot(context.T, grad_rows, preferred_element_type=jnp.float32)
    share_rows = width // seq_count
    parts = jnp.concatenate([qkv_part, out_part], axis=1).astype(jnp.bfloat16)
    gathered = lax.all_to_all(
        parts.reshape(seq_count, share_rows, parts.shape[1]), "seq", split_axis=0, concat_axis=0, tiled=True
    )
    qkv_rows = (
        jnp.sum(gathered[:, :, : 3 * head_size].astype(jnp.float32).reshape(H, groups, share_rows, 3 * head_size), axis=1)
        .reshape(H, share_rows, 3, head_size)
        .transpose(1, 2, 0, 3)
        .reshape(share_rows, 3 * width)
    )
    out_rows = jnp.sum(gathered[:, :, 3 * head_size :].astype(jnp.float32), axis=0)
    batch_count = lax.axis_size("batch")
    piece_rows = share_rows // batch_count
    shares = jnp.concatenate([qkv_rows, out_rows], axis=1).astype(jnp.bfloat16)
    pieces = lax.all_to_all(
        shares.reshape(batch_count, piece_rows, shares.shape[1]), "batch", split_axis=0, concat_axis=0, tiled=True
    )
    summed = jnp.sum(pieces.astype(jnp.float32), axis=0)
    summed = lax.all_gather(summed, "batch", axis=0, tiled=True)
    grad_qkv = summed[:, : 3 * width]
    grad_out = summed[:, 3 * width :]
    dnormed = jnp.dot(dqkv, w_qkv.T, preferred_element_type=jnp.float32)
    unused, pull = jax.vjp(layer_norm, inputs)
    grad_input = (cotangent[0].astype(jnp.float32) + pull(dnormed)[0]).astype(jnp.bfloat16)
    return (output[None], grad_input[None], grad_qkv, grad_out)


def solution(mesh):
    return jax.shard_map(
        per_device,
        mesh=mesh,
        in_specs=(P("batch", "seq", None), P("batch"), P(), P(), P("batch", "seq", None)),
        out_specs=(
            P("batch", "seq", None),
            P("batch", "seq", None),
            P("seq", None),
            P("seq", None),
        ),
        check_vma=False,
    )
```

```python
import jax
import jax.numpy as jnp
from jax import lax
from jax.sharding import PartitionSpec as P
from jax.experimental import pallas as pl
from jax.experimental.pallas import tpu as pltpu
import functools

H = 8


def from_partner(array, axis, stride):
    return lax.ppermute(array, axis, [(i, i ^ 1 << stride) for i in range(lax.axis_size(axis))])


def layer_norm(values):
    mean = jnp.mean(values, axis=-1, keepdims=True)
    centred = values - mean
    var = jnp.mean(centred * centred, axis=-1, keepdims=True)
    return centred * lax.rsqrt(var + 1e-05)


def _attn_kernel(q_ref, do_ref, k_ref, v_ref, bias_ref, ctx_ref, dq_ref, dk_ref, dv_ref, *, scale):
    i = pl.program_id(0)

    @pl.when(i == 0)
    def _():
        dk_ref[...] = jnp.zeros_like(dk_ref)
        dv_ref[...] = jnp.zeros_like(dv_ref)

    nb, rows, hd = q_ref.shape
    ns, kr, _ = k_ref.shape
    q = q_ref[...].reshape(nb * rows, hd)
    do = do_ref[...].reshape(nb * rows, hd)
    k = k_ref[...].reshape(ns * kr, hd)
    v = v_ref[...].reshape(ns * kr, hd)
    nt = (((1,), (1,)), ((), ()))
    tn = (((0,), (0,)), ((), ()))
    s = lax.dot_general(q, k, nt, preferred_element_type=jnp.float32) * scale + bias_ref[...]
    m = jnp.max(s, axis=1, keepdims=True)
    e = jnp.exp(s - m)
    p = e / jnp.sum(e, axis=1, keepdims=True)
    p16 = p.astype(jnp.bfloat16)
    ctx = jnp.dot(p16, v, preferred_element_type=jnp.float32)
    ctx_ref[...] = ctx.reshape(nb, rows, hd).astype(ctx_ref.dtype)
    dp = lax.dot_general(do, v, nt, preferred_element_type=jnp.float32)
    delta = jnp.sum(p * dp, axis=1, keepdims=True)
    ds = (p * (dp - delta)).astype(jnp.bfloat16)
    dq = jnp.dot(ds, k, preferred_element_type=jnp.float32) * scale
    dq_ref[...] = dq.reshape(nb, rows, hd).astype(dq_ref.dtype)
    dk_ref[...] += lax.dot_general(ds, q, tn, preferred_element_type=jnp.float32) * scale
    dv_ref[...] += lax.dot_general(p16, do, tn, preferred_element_type=jnp.float32)


def attn_pass(recv, part_rows, bias, scale, block_sources=4):
    sources, _, hd = recv.shape
    key_rows = 2 * part_rows
    nq = sources * part_rows
    nk = sources * key_rows
    kernel = functools.partial(_attn_kernel, scale=scale)
    return pl.pallas_call(
        kernel,
        grid=(sources // block_sources,),
        in_specs=[
            pl.BlockSpec((block_sources, part_rows, hd), lambda i: (i, 0, 0)),
            pl.BlockSpec((block_sources, part_rows, hd), lambda i: (i, 1, 0)),
            pl.BlockSpec((sources, key_rows, hd), lambda i: (0, 1, 0)),
            pl.BlockSpec((sources, key_rows, hd), lambda i: (0, 2, 0)),
            pl.BlockSpec((1, nk), lambda i: (0, 0)),
        ],
        out_specs=[
            pl.BlockSpec((block_sources, part_rows, hd), lambda i: (i, 0, 0)),
            pl.BlockSpec((block_sources, part_rows, hd), lambda i: (i, 0, 0)),
            pl.BlockSpec((nk, hd), lambda i: (0, 0)),
            pl.BlockSpec((nk, hd), lambda i: (0, 0)),
        ],
        out_shape=[
            jax.ShapeDtypeStruct((sources, part_rows, hd), jnp.bfloat16),
            jax.ShapeDtypeStruct((sources, part_rows, hd), jnp.bfloat16),
            jax.ShapeDtypeStruct((nk, hd), jnp.float32),
            jax.ShapeDtypeStruct((nk, hd), jnp.float32),
        ],
        compiler_params=pltpu.CompilerParams(dimension_semantics=("arbitrary",)),
    )(recv, recv, recv, recv, bias.reshape(1, nk))


def per_device(frames, lengths, w_qkv, w_out, cotangent):
    width = w_out.shape[0]
    head_size = width // H
    scale = float(head_size) ** (-0.5)
    tok_rows = frames.shape[1]
    seq_count = lax.axis_size("seq")
    groups = seq_count // H
    part_rows = tok_rows // groups
    frame_total = tok_rows * seq_count
    group_index = lax.axis_index("seq") % groups
    length = lengths[0]
    inputs = frames[0].astype(jnp.float32)
    normed = layer_norm(inputs).astype(jnp.bfloat16)
    qkv = jnp.dot(normed, w_qkv, preferred_element_type=jnp.float32).astype(jnp.bfloat16)
    qkv_local = qkv.reshape(tok_rows, 3, H, head_size)
    offset = lax.axis_index("seq") * tok_rows
    own_pos = offset + jnp.arange(tok_rows, dtype=jnp.int32)
    valid = (own_pos < length).astype(jnp.float32)
    grad_rows = (cotangent[0].astype(jnp.float32) * valid[:, None]).astype(jnp.bfloat16)
    dcontext = jnp.dot(grad_rows, w_out.T, preferred_element_type=jnp.float32).astype(jnp.bfloat16)

    def by_half(rows_heads):
        return rows_heads.reshape(groups, part_rows, H, head_size).transpose(2, 0, 1, 3).reshape(
            seq_count, part_rows, head_size
        )

    def to_both(rows_heads):
        both = jnp.broadcast_to(rows_heads.transpose(1, 0, 2)[:, None], (H, groups, tok_rows, head_size))
        return both.reshape(seq_count, tok_rows, head_size)

    send = jnp.concatenate(
        [
            by_half(qkv_local[:, 0]),
            by_half(dcontext.reshape(tok_rows, H, head_size)),
            to_both(qkv_local[:, 1]),
            to_both(qkv_local[:, 2]),
        ],
        axis=1,
    )
    recv = lax.all_to_all(send, "seq", split_axis=0, concat_axis=0, tiled=True)
    normed_send = jnp.broadcast_to(normed.reshape(1, groups, part_rows, width), (H, groups, part_rows, width))
    normed_recv = lax.all_to_all(
        normed_send.reshape(seq_count, part_rows, width), "seq", split_axis=0, concat_axis=0, tiled=True
    )
    position = jnp.arange(frame_total, dtype=jnp.int32)
    bias = jnp.where(position < length, 0.0, -1000000000.0).astype(jnp.float32)

    context_h, dquery, dkeys, dvalues = attn_pass(recv, part_rows, bias, scale)

    split_grads = jnp.stack([dkeys, dvalues], axis=1).reshape(seq_count, groups, part_rows, 2, head_size)
    own_half = lax.dynamic_index_in_dim(split_grads, group_index, 1, keepdims=False)
    other_half = lax.dynamic_index_in_dim(split_grads, 1 - group_index, 1, keepdims=False)
    partner_half = from_partner(other_half.astype(jnp.bfloat16), "seq", 0)
    paired_rows = (own_half + partner_half.astype(jnp.float32)).astype(jnp.bfloat16)
    back = jnp.concatenate(
        [
            context_h.reshape(seq_count, part_rows, 1, head_size),
            dquery.reshape(seq_count, part_rows, 1, head_size),
            paired_rows,
        ],
        axis=2,
    )
    returned = lax.all_to_all(back, "seq", split_axis=0, concat_axis=0, tiled=True)
    returned = returned.reshape(H, groups, part_rows, 4, head_size).transpose(1, 2, 3, 0, 4)
    context = returned[:, :, 0].reshape(tok_rows, width)
    dqkv = returned[:, :, 1:].reshape(tok_rows, 3 * width)
    branch = jnp.dot(context, w_out, preferred_element_type=jnp.float32)
    output = (inputs + valid[:, None] * branch).astype(jnp.bfloat16)
    over_frames = (((0, 1), (0, 1)), ((), ()))
    qkv_part = lax.dot_general(
        normed_recv, back[:, :, 1:], over_frames, preferred_element_type=jnp.float32
    ).reshape(width, 3 * head_size)
    out_part = jnp.dot(context.T, grad_rows, preferred_element_type=jnp.float32)
    share_rows = width // seq_count
    parts = jnp.concatenate([qkv_part, out_part], axis=1).astype(jnp.bfloat16)
    gathered = lax.all_to_all(
        parts.reshape(seq_count, share_rows, parts.shape[1]), "seq", split_axis=0, concat_axis=0, tiled=True
    )
    qkv_rows = (
        jnp.sum(gathered[:, :, : 3 * head_size].astype(jnp.float32).reshape(H, groups, share_rows, 3 * head_size), axis=1)
        .reshape(H, share_rows, 3, head_size)
        .transpose(1, 2, 0, 3)
        .reshape(share_rows, 3 * width)
    )
    out_rows = jnp.sum(gathered[:, :, 3 * head_size :].astype(jnp.float32), axis=0)
    batch_count = lax.axis_size("batch")
    piece_rows = share_rows // batch_count
    shares = jnp.concatenate([qkv_rows, out_rows], axis=1).astype(jnp.bfloat16)
    pieces = lax.all_to_all(
        shares.reshape(batch_count, piece_rows, shares.shape[1]), "batch", split_axis=0, concat_axis=0, tiled=True
    )
    summed = jnp.sum(pieces.astype(jnp.float32), axis=0)
    summed = lax.all_gather(summed, "batch", axis=0, tiled=True)
    grad_qkv = summed[:, : 3 * width]
    grad_out = summed[:, 3 * width :]
    dnormed = jnp.dot(dqkv, w_qkv.T, preferred_element_type=jnp.float32)
    unused, pull = jax.vjp(layer_norm, inputs)
    grad_input = (cotangent[0].astype(jnp.float32) + pull(dnormed)[0]).astype(jnp.bfloat16)
    return (output[None], grad_input[None], grad_qkv, grad_out)


def solution(mesh):
    return jax.shard_map(
        per_device,
        mesh=mesh,
        in_specs=(P("batch", "seq", None), P("batch"), P(), P(), P("batch", "seq", None)),
        out_specs=(
            P("batch", "seq", None),
            P("batch", "seq", None),
            P("seq", None),
            P("seq", None),
        ),
        check_vma=False,
    )
```

```python
import jax
import jax.numpy as jnp
from jax import lax
from jax.sharding import PartitionSpec as P
from jax.experimental import pallas as pl
from jax.experimental.pallas import tpu as pltpu
import functools

H = 8


def from_partner(array, axis, stride):
    return lax.ppermute(array, axis, [(i, i ^ 1 << stride) for i in range(lax.axis_size(axis))])


def layer_norm(values):
    mean = jnp.mean(values, axis=-1, keepdims=True)
    centred = values - mean
    var = jnp.mean(centred * centred, axis=-1, keepdims=True)
    return centred * lax.rsqrt(var + 1e-05)


def _attn_kernel(q_ref, do_ref, k_ref, v_ref, bias_ref, ctx_ref, dq_ref, dk_ref, dv_ref, *, scale):
    i = pl.program_id(0)

    @pl.when(i == 0)
    def _():
        dk_ref[...] = jnp.zeros_like(dk_ref)
        dv_ref[...] = jnp.zeros_like(dv_ref)

    nb, rows, hd = q_ref.shape
    ns, kr, _ = k_ref.shape
    q = q_ref[...].reshape(nb * rows, hd)
    do = do_ref[...].reshape(nb * rows, hd)
    k = k_ref[...].reshape(ns * kr, hd)
    v = v_ref[...].reshape(ns * kr, hd)
    nt = (((1,), (1,)), ((), ()))
    tn = (((0,), (0,)), ((), ()))
    s = lax.dot_general(q, k, nt, preferred_element_type=jnp.float32) * scale + bias_ref[...]
    m = jnp.max(s, axis=1, keepdims=True)
    e = jnp.exp(s - m)
    p = e / jnp.sum(e, axis=1, keepdims=True)
    p16 = p.astype(jnp.bfloat16)
    ctx = jnp.dot(p16, v, preferred_element_type=jnp.float32)
    ctx_ref[...] = ctx.reshape(nb, rows, hd).astype(ctx_ref.dtype)
    dp = lax.dot_general(do, v, nt, preferred_element_type=jnp.float32)
    delta = jnp.sum(p * dp, axis=1, keepdims=True)
    ds = (p * (dp - delta)).astype(jnp.bfloat16)
    dq = jnp.dot(ds, k, preferred_element_type=jnp.float32) * scale
    dq_ref[...] = dq.reshape(nb, rows, hd).astype(dq_ref.dtype)
    dk_ref[...] += lax.dot_general(ds, q, tn, preferred_element_type=jnp.float32) * scale
    dv_ref[...] += lax.dot_general(p16, do, tn, preferred_element_type=jnp.float32)


def attn_pass(recv, part_rows, bias, scale, block_sources=4):
    sources, _, hd = recv.shape
    key_rows = 2 * part_rows
    nq = sources * part_rows
    nk = sources * key_rows
    kernel = functools.partial(_attn_kernel, scale=scale)
    return pl.pallas_call(
        kernel,
        grid=(sources // block_sources,),
        in_specs=[
            pl.BlockSpec((block_sources, part_rows, hd), lambda i: (i, 0, 0)),
            pl.BlockSpec((block_sources, part_rows, hd), lambda i: (i, 1, 0)),
            pl.BlockSpec((sources, key_rows, hd), lambda i: (0, 1, 0)),
            pl.BlockSpec((sources, key_rows, hd), lambda i: (0, 2, 0)),
            pl.BlockSpec((1, nk), lambda i: (0, 0)),
        ],
        out_specs=[
            pl.BlockSpec((block_sources, part_rows, hd), lambda i: (i, 0, 0)),
            pl.BlockSpec((block_sources, part_rows, hd), lambda i: (i, 0, 0)),
            pl.BlockSpec((nk, hd), lambda i: (0, 0)),
            pl.BlockSpec((nk, hd), lambda i: (0, 0)),
        ],
        out_shape=[
            jax.ShapeDtypeStruct((sources, part_rows, hd), jnp.bfloat16),
            jax.ShapeDtypeStruct((sources, part_rows, hd), jnp.bfloat16),
            jax.ShapeDtypeStruct((nk, hd), jnp.float32),
            jax.ShapeDtypeStruct((nk, hd), jnp.float32),
        ],
        compiler_params=pltpu.CompilerParams(dimension_semantics=("arbitrary",)),
    )(recv, recv, recv, recv, bias.reshape(1, nk))


def per_device(frames, lengths, w_qkv, w_out, cotangent):
    width = w_out.shape[0]
    head_size = width // H
    scale = float(head_size) ** (-0.5)
    tok_rows = frames.shape[1]
    seq_count = lax.axis_size("seq")
    groups = seq_count // H
    part_rows = tok_rows // groups
    frame_total = tok_rows * seq_count
    group_index = lax.axis_index("seq") % groups
    length = lengths[0]
    inputs = frames[0].astype(jnp.float32)
    normed = layer_norm(inputs).astype(jnp.bfloat16)
    qkv = jnp.dot(normed, w_qkv, preferred_element_type=jnp.float32).astype(jnp.bfloat16)
    qkv_local = qkv.reshape(tok_rows, 3, H, head_size)
    offset = lax.axis_index("seq") * tok_rows
    own_pos = offset + jnp.arange(tok_rows, dtype=jnp.int32)
    valid = (own_pos < length).astype(jnp.float32)
    grad_rows = (cotangent[0].astype(jnp.float32) * valid[:, None]).astype(jnp.bfloat16)
    dcontext = jnp.dot(grad_rows, w_out.T, preferred_element_type=jnp.float32).astype(jnp.bfloat16)

    def by_half(rows_heads):
        return rows_heads.reshape(groups, part_rows, H, head_size).transpose(2, 0, 1, 3).reshape(
            seq_count, part_rows, head_size
        )

    def to_both(rows_heads):
        both = jnp.broadcast_to(rows_heads.transpose(1, 0, 2)[:, None], (H, groups, tok_rows, head_size))
        return both.reshape(seq_count, tok_rows, head_size)

    send = jnp.concatenate(
        [
            by_half(qkv_local[:, 0]),
            by_half(dcontext.reshape(tok_rows, H, head_size)),
            to_both(qkv_local[:, 1]),
            to_both(qkv_local[:, 2]),
        ],
        axis=1,
    )
    recv = lax.all_to_all(send, "seq", split_axis=0, concat_axis=0, tiled=True)
    normed_send = jnp.broadcast_to(normed.reshape(1, groups, part_rows, width), (H, groups, part_rows, width))
    normed_recv = lax.all_to_all(
        normed_send.reshape(seq_count, part_rows, width), "seq", split_axis=0, concat_axis=0, tiled=True
    )
    position = jnp.arange(frame_total, dtype=jnp.int32)
    bias = jnp.where(position < length, 0.0, -1000000000.0).astype(jnp.float32)

    context_h, dquery, dkeys, dvalues = attn_pass(recv, part_rows, bias, scale)

    batch_count = lax.axis_size("batch")
    share_rows = width // seq_count
    piece_rows = share_rows // batch_count
    context_back = lax.all_to_all(context_h, "seq", split_axis=0, concat_axis=0, tiled=True)
    context = context_back.reshape(H, groups, part_rows, head_size).transpose(1, 2, 0, 3).reshape(tok_rows, width)
    branch = jnp.dot(context, w_out, preferred_element_type=jnp.float32)
    output = (inputs + valid[:, None] * branch).astype(jnp.bfloat16)
    out_part = jnp.dot(context.T, grad_rows, preferred_element_type=jnp.float32).astype(jnp.bfloat16)
    out_part = out_part.reshape(seq_count, batch_count, piece_rows, width).transpose(1, 0, 2, 3)
    out_batch = lax.psum_scatter(out_part.reshape(width, width), "batch", scatter_dimension=0, tiled=True)

    split_grads = jnp.stack([dkeys, dvalues], axis=1).reshape(seq_count, groups, part_rows, 2, head_size)
    own_half = lax.dynamic_index_in_dim(split_grads, group_index, 1, keepdims=False)
    other_half = lax.dynamic_index_in_dim(split_grads, 1 - group_index, 1, keepdims=False)
    partner_half = from_partner(other_half.astype(jnp.bfloat16), "seq", 0)
    paired_rows = (own_half + partner_half.astype(jnp.float32)).astype(jnp.bfloat16)
    back = jnp.concatenate([dquery.reshape(seq_count, part_rows, 1, head_size), paired_rows], axis=2)
    returned = lax.all_to_all(back, "seq", split_axis=0, concat_axis=0, tiled=True)
    dqkv = returned.reshape(H, groups, part_rows, 3, head_size).transpose(1, 2, 3, 0, 4).reshape(tok_rows, 3 * width)
    over_frames = (((0, 1), (0, 1)), ((), ()))
    qkv_part = lax.dot_general(normed_recv, back, over_frames, preferred_element_type=jnp.float32)
    qkv_send = qkv_part.astype(jnp.bfloat16).reshape(seq_count, share_rows * 3 * head_size)
    out_send = out_batch.reshape(seq_count, piece_rows * width)
    gathered = lax.all_to_all(
        jnp.concatenate([qkv_send, out_send], axis=1), "seq", split_axis=0, concat_axis=0, tiled=True
    )
    qkv_split = share_rows * 3 * head_size
    qkv_rows = (
        jnp.sum(gathered[:, :qkv_split].astype(jnp.float32).reshape(H, groups, share_rows, 3 * head_size), axis=1)
        .reshape(H, share_rows, 3, head_size)
        .transpose(1, 2, 0, 3)
        .reshape(share_rows, 3 * width)
    )
    out_rows = jnp.sum(gathered[:, qkv_split:].astype(jnp.float32).reshape(seq_count, piece_rows, width), axis=0)
    pieces = lax.all_to_all(
        qkv_rows.astype(jnp.bfloat16).reshape(batch_count, piece_rows, 3 * width),
        "batch",
        split_axis=0,
        concat_axis=0,
        tiled=True,
    )
    qkv_sum = jnp.sum(pieces.astype(jnp.float32), axis=0)
    summed = lax.all_gather(jnp.concatenate([qkv_sum, out_rows], axis=1), "batch", axis=0, tiled=True)
    grad_qkv = summed[:, : 3 * width]
    grad_out = summed[:, 3 * width :]
    dnormed = jnp.dot(dqkv, w_qkv.T, preferred_element_type=jnp.float32)
    unused, pull = jax.vjp(layer_norm, inputs)
    grad_input = (cotangent[0].astype(jnp.float32) + pull(dnormed)[0]).astype(jnp.bfloat16)
    return (output[None], grad_input[None], grad_qkv, grad_out)


def solution(mesh):
    return jax.shard_map(
        per_device,
        mesh=mesh,
        in_specs=(P("batch", "seq", None), P("batch"), P(), P(), P("batch", "seq", None)),
        out_specs=(
            P("batch", "seq", None),
            P("batch", "seq", None),
            P("seq", None),
            P("seq", None),
        ),
        check_vma=False,
    )
```

```python
import jax
import jax.numpy as jnp
from jax import lax
from jax.sharding import PartitionSpec as P
from jax.experimental import pallas as pl
from jax.experimental.pallas import tpu as pltpu
import functools

H = 8


def from_partner(array, axis, stride):
    return lax.ppermute(array, axis, [(i, i ^ 1 << stride) for i in range(lax.axis_size(axis))])


def layer_norm(values):
    mean = jnp.mean(values, axis=-1, keepdims=True)
    centred = values - mean
    var = jnp.mean(centred * centred, axis=-1, keepdims=True)
    return centred * lax.rsqrt(var + 1e-05)


def _attn_kernel(q_ref, do_ref, k_ref, v_ref, bias_ref, ctx_ref, dq_ref, dk_ref, dv_ref, *, scale):
    i = pl.program_id(0)

    @pl.when(i == 0)
    def _():
        dk_ref[...] = jnp.zeros_like(dk_ref)
        dv_ref[...] = jnp.zeros_like(dv_ref)

    nb, rows, hd = q_ref.shape
    ns, kr, _ = k_ref.shape
    q = q_ref[...].reshape(nb * rows, hd)
    do = do_ref[...].reshape(nb * rows, hd)
    k = k_ref[...].reshape(ns * kr, hd)
    v = v_ref[...].reshape(ns * kr, hd)
    nt = (((1,), (1,)), ((), ()))
    tn = (((0,), (0,)), ((), ()))
    s = lax.dot_general(q, k, nt, preferred_element_type=jnp.float32) * scale + bias_ref[...]
    m = jnp.max(s, axis=1, keepdims=True)
    e = jnp.exp(s - m)
    p = e / jnp.sum(e, axis=1, keepdims=True)
    p16 = p.astype(jnp.bfloat16)
    ctx = jnp.dot(p16, v, preferred_element_type=jnp.float32)
    ctx_ref[...] = ctx.reshape(nb, rows, hd).astype(ctx_ref.dtype)
    dp = lax.dot_general(do, v, nt, preferred_element_type=jnp.float32)
    delta = jnp.sum(p * dp, axis=1, keepdims=True)
    ds = (p * (dp - delta)).astype(jnp.bfloat16)
    dq = jnp.dot(ds, k, preferred_element_type=jnp.float32) * scale
    dq_ref[...] = dq.reshape(nb, rows, hd).astype(dq_ref.dtype)
    dk_ref[...] += lax.dot_general(ds, q, tn, preferred_element_type=jnp.float32) * scale
    dv_ref[...] += lax.dot_general(p16, do, tn, preferred_element_type=jnp.float32)


def attn_pass(recv, part_rows, bias, scale, block_sources=4):
    sources, _, hd = recv.shape
    key_rows = 2 * part_rows
    nk = sources * key_rows
    kernel = functools.partial(_attn_kernel, scale=scale)
    return pl.pallas_call(
        kernel,
        grid=(sources // block_sources,),
        in_specs=[
            pl.BlockSpec((block_sources, part_rows, hd), lambda i: (i, 0, 0)),
            pl.BlockSpec((block_sources, part_rows, hd), lambda i: (i, 1, 0)),
            pl.BlockSpec((sources, key_rows, hd), lambda i: (0, 1, 0)),
            pl.BlockSpec((sources, key_rows, hd), lambda i: (0, 2, 0)),
            pl.BlockSpec((1, nk), lambda i: (0, 0)),
        ],
        out_specs=[
            pl.BlockSpec((block_sources, part_rows, hd), lambda i: (i, 0, 0)),
            pl.BlockSpec((block_sources, part_rows, hd), lambda i: (i, 0, 0)),
            pl.BlockSpec((nk, hd), lambda i: (0, 0)),
            pl.BlockSpec((nk, hd), lambda i: (0, 0)),
        ],
        out_shape=[
            jax.ShapeDtypeStruct((sources, part_rows, hd), jnp.bfloat16),
            jax.ShapeDtypeStruct((sources, part_rows, hd), jnp.bfloat16),
            jax.ShapeDtypeStruct((nk, hd), jnp.float32),
            jax.ShapeDtypeStruct((nk, hd), jnp.float32),
        ],
        compiler_params=pltpu.CompilerParams(dimension_semantics=("arbitrary",)),
    )(recv, recv, recv, recv, bias.reshape(1, nk))


def device_body(frames, lengths, w_qkv, w_out, cotangent):
    width = w_out.shape[0]
    head_size = width // H
    scale = float(head_size) ** (-0.5)
    tok_rows = frames.shape[1]
    seq_count = lax.axis_size("seq")
    groups = seq_count // H
    part_rows = tok_rows // groups
    frame_total = tok_rows * seq_count
    group_index = lax.axis_index("seq") % groups
    length = lengths[0]
    inputs = frames[0].astype(jnp.float32)
    normed = layer_norm(inputs).astype(jnp.bfloat16)
    qkv = jnp.dot(normed, w_qkv, preferred_element_type=jnp.float32).astype(jnp.bfloat16)
    qkv_local = qkv.reshape(tok_rows, 3, H, head_size)
    offset = lax.axis_index("seq") * tok_rows
    own_pos = offset + jnp.arange(tok_rows, dtype=jnp.int32)
    valid = (own_pos < length).astype(jnp.float32)
    grad_rows = (cotangent[0].astype(jnp.float32) * valid[:, None]).astype(jnp.bfloat16)
    dcontext = jnp.dot(grad_rows, w_out.T, preferred_element_type=jnp.float32).astype(jnp.bfloat16)

    def by_half(rows_heads):
        return rows_heads.reshape(groups, part_rows, H, head_size).transpose(2, 0, 1, 3).reshape(
            seq_count, part_rows, head_size
        )

    def to_both(rows_heads):
        both = jnp.broadcast_to(rows_heads.transpose(1, 0, 2)[:, None], (H, groups, tok_rows, head_size))
        return both.reshape(seq_count, tok_rows, head_size)

    send = jnp.concatenate(
        [
            by_half(qkv_local[:, 0]),
            by_half(dcontext.reshape(tok_rows, H, head_size)),
            to_both(qkv_local[:, 1]),
            to_both(qkv_local[:, 2]),
        ],
        axis=1,
    )
    recv = lax.all_to_all(send, "seq", split_axis=0, concat_axis=0, tiled=True)
    normed_send = jnp.broadcast_to(normed.reshape(1, groups, part_rows, width), (H, groups, part_rows, width))
    normed_recv = lax.all_to_all(
        normed_send.reshape(seq_count, part_rows, width), "seq", split_axis=0, concat_axis=0, tiled=True
    )
    position = jnp.arange(frame_total, dtype=jnp.int32)
    bias = jnp.where(position < length, 0.0, -1000000000.0).astype(jnp.float32)

    context_h, dquery, dkeys, dvalues = attn_pass(recv, part_rows, bias, scale)

    split_grads = jnp.stack([dkeys, dvalues], axis=1).reshape(seq_count, groups, part_rows, 2, head_size)
    own_half = lax.dynamic_index_in_dim(split_grads, group_index, 1, keepdims=False)
    other_half = lax.dynamic_index_in_dim(split_grads, 1 - group_index, 1, keepdims=False)
    partner_half = from_partner(other_half.astype(jnp.bfloat16), "seq", 0)
    paired_rows = (own_half + partner_half.astype(jnp.float32)).astype(jnp.bfloat16)
    back = jnp.concatenate(
        [
            context_h.reshape(seq_count, part_rows, 1, head_size),
            dquery.reshape(seq_count, part_rows, 1, head_size),
            paired_rows,
        ],
        axis=2,
    )
    returned = lax.all_to_all(back, "seq", split_axis=0, concat_axis=0, tiled=True)
    returned = returned.reshape(H, groups, part_rows, 4, head_size).transpose(1, 2, 3, 0, 4)
    context = returned[:, :, 0].reshape(tok_rows, width)
    dqkv = returned[:, :, 1:].reshape(tok_rows, 3 * width)
    branch = jnp.dot(context, w_out, preferred_element_type=jnp.float32)
    output = (inputs + valid[:, None] * branch).astype(jnp.bfloat16)
    over_frames = (((0, 1), (0, 1)), ((), ()))
    qkv_part = lax.dot_general(
        normed_recv, back[:, :, 1:], over_frames, preferred_element_type=jnp.float32
    ).reshape(width, 3 * head_size)
    out_part = jnp.dot(context.T, grad_rows, preferred_element_type=jnp.float32)
    share_rows = width // seq_count
    parts = jnp.concatenate([qkv_part, out_part], axis=1).astype(jnp.bfloat16)
    gathered = lax.all_to_all(
        parts.reshape(seq_count, share_rows, parts.shape[1]), "seq", split_axis=0, concat_axis=0, tiled=True
    )
    qkv_rows = (
        jnp.sum(gathered[:, :, : 3 * head_size].astype(jnp.float32).reshape(H, groups, share_rows, 3 * head_size), axis=1)
        .reshape(H, share_rows, 3, head_size)
        .transpose(1, 2, 0, 3)
        .reshape(share_rows, 3 * width)
    )
    out_rows = jnp.sum(gathered[:, :, 3 * head_size :].astype(jnp.float32), axis=0)
    batch_count = lax.axis_size("batch")
    piece_rows = share_rows // batch_count
    shares = jnp.concatenate([qkv_rows, out_rows], axis=1).astype(jnp.bfloat16)
    pieces = lax.all_to_all(
        shares.reshape(batch_count, piece_rows, shares.shape[1]), "batch", split_axis=0, concat_axis=0, tiled=True
    )
    summed = jnp.sum(pieces.astype(jnp.float32), axis=0)
    summed = lax.all_gather(summed, "batch", axis=0, tiled=True)
    grad_qkv = summed[:, : 3 * width]
    grad_out = summed[:, 3 * width :]
    dnormed = jnp.dot(dqkv, w_qkv.T, preferred_element_type=jnp.float32)
    _, pull = jax.vjp(layer_norm, inputs)
    grad_input = (cotangent[0].astype(jnp.float32) + pull(dnormed)[0]).astype(jnp.bfloat16)
    return (output[None], grad_input[None], grad_qkv, grad_out)


def solution(mesh):
    return jax.shard_map(
        device_body,
        mesh=mesh,
        in_specs=(P("batch", "seq", None), P("batch"), P(), P(), P("batch", "seq", None)),
        out_specs=(
            P("batch", "seq", None),
            P("batch", "seq", None),
            P("seq", None),
            P("seq", None),
        ),
        check_vma=False,
    )
```

```python
import jax
import jax.numpy as jnp
from jax import lax
from jax.sharding import PartitionSpec as P
from jax.experimental import pallas as pl
from jax.experimental.pallas import tpu as pltpu
import functools

H = 8


def from_partner(array, axis, stride):
    return lax.ppermute(array, axis, [(i, i ^ 1 << stride) for i in range(lax.axis_size(axis))])


def layer_norm(values):
    mean = jnp.mean(values, axis=-1, keepdims=True)
    centred = values - mean
    var = jnp.mean(centred * centred, axis=-1, keepdims=True)
    return centred * lax.rsqrt(var + 1e-05)


def _attn_kernel(q_ref, do_ref, k_ref, v_ref, bias_ref, ctx_ref, dq_ref, dk_ref, dv_ref, *, scale):
    i = pl.program_id(0)

    @pl.when(i == 0)
    def _():
        dk_ref[...] = jnp.zeros_like(dk_ref)
        dv_ref[...] = jnp.zeros_like(dv_ref)

    nb, rows, hd = q_ref.shape
    ns, kr, _ = k_ref.shape
    q = q_ref[...].reshape(nb * rows, hd)
    do = do_ref[...].reshape(nb * rows, hd)
    k = k_ref[...].reshape(ns * kr, hd)
    v = v_ref[...].reshape(ns * kr, hd)
    nt = (((1,), (1,)), ((), ()))
    tn = (((0,), (0,)), ((), ()))
    s = lax.dot_general(q, k, nt, preferred_element_type=jnp.float32) * scale + bias_ref[...]
    m = jnp.max(s, axis=1, keepdims=True)
    e = jnp.exp(s - m)
    p = e / jnp.sum(e, axis=1, keepdims=True)
    p16 = p.astype(jnp.bfloat16)
    ctx = jnp.dot(p16, v, preferred_element_type=jnp.float32)
    ctx_ref[...] = ctx.reshape(nb, rows, hd).astype(ctx_ref.dtype)
    dp = lax.dot_general(do, v, nt, preferred_element_type=jnp.float32)
    delta = jnp.sum(p * dp, axis=1, keepdims=True)
    ds = (p * (dp - delta)).astype(jnp.bfloat16)
    dq = jnp.dot(ds, k, preferred_element_type=jnp.float32) * scale
    dq_ref[...] = dq.reshape(nb, rows, hd).astype(dq_ref.dtype)
    dk_ref[...] += lax.dot_general(ds, q, tn, preferred_element_type=jnp.float32) * scale
    dv_ref[...] += lax.dot_general(p16, do, tn, preferred_element_type=jnp.float32)


def attn_pass(recv, part_rows, bias, scale, block_sources=4):
    sources, _, hd = recv.shape
    key_rows = 2 * part_rows
    nq = sources * part_rows
    nk = sources * key_rows
    kernel = functools.partial(_attn_kernel, scale=scale)
    return pl.pallas_call(
        kernel,
        grid=(sources // block_sources,),
        in_specs=[
            pl.BlockSpec((block_sources, part_rows, hd), lambda i: (i, 0, 0)),
            pl.BlockSpec((block_sources, part_rows, hd), lambda i: (i, 1, 0)),
            pl.BlockSpec((sources, key_rows, hd), lambda i: (0, 1, 0)),
            pl.BlockSpec((sources, key_rows, hd), lambda i: (0, 2, 0)),
            pl.BlockSpec((1, nk), lambda i: (0, 0)),
        ],
        out_specs=[
            pl.BlockSpec((block_sources, part_rows, hd), lambda i: (i, 0, 0)),
            pl.BlockSpec((block_sources, part_rows, hd), lambda i: (i, 0, 0)),
            pl.BlockSpec((nk, hd), lambda i: (0, 0)),
            pl.BlockSpec((nk, hd), lambda i: (0, 0)),
        ],
        out_shape=[
            jax.ShapeDtypeStruct((sources, part_rows, hd), jnp.bfloat16),
            jax.ShapeDtypeStruct((sources, part_rows, hd), jnp.bfloat16),
            jax.ShapeDtypeStruct((nk, hd), jnp.float32),
            jax.ShapeDtypeStruct((nk, hd), jnp.float32),
        ],
        compiler_params=pltpu.CompilerParams(dimension_semantics=("arbitrary",)),
    )(recv, recv, recv, recv, bias.reshape(1, nk))


def per_device(frames, lengths, w_qkv, w_out, cotangent):
    width = w_out.shape[0]
    head_size = width // H
    scale = float(head_size) ** (-0.5)
    tok_rows = frames.shape[1]
    seq_count = lax.axis_size("seq")
    groups = seq_count // H
    part_rows = tok_rows // groups
    frame_total = tok_rows * seq_count
    group_index = lax.axis_index("seq") % groups
    length = lengths[0]
    inputs = frames[0].astype(jnp.float32)
    normed = layer_norm(inputs).astype(jnp.bfloat16)
    qkv = jnp.dot(normed, w_qkv, preferred_element_type=jnp.float32).astype(jnp.bfloat16)
    qkv_local = qkv.reshape(tok_rows, 3, H, head_size)
    offset = lax.axis_index("seq") * tok_rows
    own_pos = offset + jnp.arange(tok_rows, dtype=jnp.int32)
    valid = (own_pos < length).astype(jnp.float32)
    grad_rows = (cotangent[0].astype(jnp.float32) * valid[:, None]).astype(jnp.bfloat16)
    dcontext = jnp.dot(grad_rows, w_out.T, preferred_element_type=jnp.float32).astype(jnp.bfloat16)

    def by_half(rows_heads):
        return rows_heads.reshape(groups, part_rows, H, head_size).transpose(2, 0, 1, 3).reshape(
            seq_count, part_rows, head_size
        )

    def to_both(rows_heads):
        both = jnp.broadcast_to(rows_heads.transpose(1, 0, 2)[:, None], (H, groups, tok_rows, head_size))
        return both.reshape(seq_count, tok_rows, head_size)

    send = jnp.concatenate(
        [
            by_half(qkv_local[:, 0]),
            by_half(dcontext.reshape(tok_rows, H, head_size)),
            to_both(qkv_local[:, 1]),
            to_both(qkv_local[:, 2]),
        ],
        axis=1,
    )
    recv = lax.all_to_all(send, "seq", split_axis=0, concat_axis=0, tiled=True)
    normed_send = jnp.broadcast_to(normed.reshape(1, groups, part_rows, width), (H, groups, part_rows, width))
    normed_recv = lax.all_to_all(
        normed_send.reshape(seq_count, part_rows, width), "seq", split_axis=0, concat_axis=0, tiled=True
    )
    position = jnp.arange(frame_total, dtype=jnp.int32)
    bias = jnp.where(position < length, 0.0, -1000000000.0).astype(jnp.float32)

    context_h, dquery, dkeys, dvalues = attn_pass(recv, part_rows, bias, scale)

    split_grads = jnp.stack([dkeys, dvalues], axis=1).reshape(seq_count, groups, part_rows, 2, head_size)
    own_half = lax.dynamic_index_in_dim(split_grads, group_index, 1, keepdims=False)
    other_half = lax.dynamic_index_in_dim(split_grads, 1 - group_index, 1, keepdims=False)
    partner_half = from_partner(other_half.astype(jnp.bfloat16), "seq", 0)
    paired_rows = (own_half + partner_half.astype(jnp.float32)).astype(jnp.bfloat16)
    back = jnp.concatenate(
        [
            context_h.reshape(seq_count, part_rows, 1, head_size),
            dquery.reshape(seq_count, part_rows, 1, head_size),
            paired_rows,
        ],
        axis=2,
    )
    returned = lax.all_to_all(back, "seq", split_axis=0, concat_axis=0, tiled=True)
    returned = returned.reshape(H, groups, part_rows, 4, head_size).transpose(1, 2, 3, 0, 4)
    context = returned[:, :, 0].reshape(tok_rows, width)
    dqkv = returned[:, :, 1:].reshape(tok_rows, 3 * width)
    branch = jnp.dot(context, w_out, preferred_element_type=jnp.float32)
    output = (inputs + valid[:, None] * branch).astype(jnp.bfloat16)
    over_frames = (((0, 1), (0, 1)), ((), ()))
    qkv_part = lax.dot_general(
        normed_recv, back[:, :, 1:], over_frames, preferred_element_type=jnp.float32
    ).reshape(width, 3 * head_size)
    out_part = jnp.dot(context.T, grad_rows, preferred_element_type=jnp.float32)
    batch_count = lax.axis_size("batch")
    piece_rows = width // (seq_count * batch_count)
    parts = jnp.concatenate([qkv_part, out_part], axis=1).astype(jnp.bfloat16)
    gathered = lax.all_to_all(
        parts.reshape(seq_count * batch_count, piece_rows, parts.shape[1]),
        ("seq", "batch"),
        split_axis=0,
        concat_axis=0,
        tiled=True,
    )
    qkv_in = gathered[:, :, : 3 * head_size].astype(jnp.float32)
    qkv_in = jnp.sum(qkv_in.reshape(H, groups * batch_count, piece_rows, 3 * head_size), axis=1)
    qkv_rows = qkv_in.reshape(H, piece_rows, 3, head_size).transpose(1, 2, 0, 3).reshape(piece_rows, 3 * width)
    out_rows = jnp.sum(gathered[:, :, 3 * head_size :].astype(jnp.float32), axis=0)
    summed = lax.all_gather(jnp.concatenate([qkv_rows, out_rows], axis=1), "batch", axis=0, tiled=True)
    grad_qkv = summed[:, : 3 * width]
    grad_out = summed[:, 3 * width :]
    dnormed = jnp.dot(dqkv, w_qkv.T, preferred_element_type=jnp.float32)
    unused, pull = jax.vjp(layer_norm, inputs)
    grad_input = (cotangent[0].astype(jnp.float32) + pull(dnormed)[0]).astype(jnp.bfloat16)
    return (output[None], grad_input[None], grad_qkv, grad_out)


def solution(mesh):
    return jax.shard_map(
        per_device,
        mesh=mesh,
        in_specs=(P("batch", "seq", None), P("batch"), P(), P(), P("batch", "seq", None)),
        out_specs=(
            P("batch", "seq", None),
            P("batch", "seq", None),
            P("seq", None),
            P("seq", None),
        ),
        check_vma=False,
    )
```

```python
import jax
import jax.numpy as jnp
from jax import lax
from jax.sharding import Mesh, PartitionSpec as P
from jax.experimental import pallas as pl
from jax.experimental.pallas import tpu as pltpu
import functools

H = 8


def from_partner(array, axis, stride):
    return lax.ppermute(array, axis, [(i, i ^ 1 << stride) for i in range(lax.axis_size(axis))])


def layer_norm(values):
    mean = jnp.mean(values, axis=-1, keepdims=True)
    centred = values - mean
    var = jnp.mean(centred * centred, axis=-1, keepdims=True)
    return centred * lax.rsqrt(var + 1e-05)


def _attn_kernel(q_ref, do_ref, k_ref, v_ref, bias_ref, ctx_ref, dq_ref, dk_ref, dv_ref, *, scale):
    i = pl.program_id(0)

    @pl.when(i == 0)
    def _():
        dk_ref[...] = jnp.zeros_like(dk_ref)
        dv_ref[...] = jnp.zeros_like(dv_ref)

    nb, rows, hd = q_ref.shape
    ns, kr, _ = k_ref.shape
    q = q_ref[...].reshape(nb * rows, hd)
    do = do_ref[...].reshape(nb * rows, hd)
    k = k_ref[...].reshape(ns * kr, hd)
    v = v_ref[...].reshape(ns * kr, hd)
    nt = (((1,), (1,)), ((), ()))
    tn = (((0,), (0,)), ((), ()))
    s = lax.dot_general(q, k, nt, preferred_element_type=jnp.float32) * scale + bias_ref[...]
    m = jnp.max(s, axis=1, keepdims=True)
    e = jnp.exp(s - m)
    p = e / jnp.sum(e, axis=1, keepdims=True)
    p16 = p.astype(jnp.bfloat16)
    ctx = jnp.dot(p16, v, preferred_element_type=jnp.float32)
    ctx_ref[...] = ctx.reshape(nb, rows, hd).astype(ctx_ref.dtype)
    dp = lax.dot_general(do, v, nt, preferred_element_type=jnp.float32)
    delta = jnp.sum(p * dp, axis=1, keepdims=True)
    ds = (p * (dp - delta)).astype(jnp.bfloat16)
    dq = jnp.dot(ds, k, preferred_element_type=jnp.float32) * scale
    dq_ref[...] = dq.reshape(nb, rows, hd).astype(dq_ref.dtype)
    dk_ref[...] += lax.dot_general(ds, q, tn, preferred_element_type=jnp.float32) * scale
    dv_ref[...] += lax.dot_general(p16, do, tn, preferred_element_type=jnp.float32)


def attn_pass(recv, part_rows, bias, scale, block_sources=4):
    sources, _, hd = recv.shape
    key_rows = 2 * part_rows
    nq = sources * part_rows
    nk = sources * key_rows
    kernel = functools.partial(_attn_kernel, scale=scale)
    return pl.pallas_call(
        kernel,
        grid=(sources // block_sources,),
        in_specs=[
            pl.BlockSpec((block_sources, part_rows, hd), lambda i: (i, 0, 0)),
            pl.BlockSpec((block_sources, part_rows, hd), lambda i: (i, 1, 0)),
            pl.BlockSpec((sources, key_rows, hd), lambda i: (0, 1, 0)),
            pl.BlockSpec((sources, key_rows, hd), lambda i: (0, 2, 0)),
            pl.BlockSpec((1, nk), lambda i: (0, 0)),
        ],
        out_specs=[
            pl.BlockSpec((block_sources, part_rows, hd), lambda i: (i, 0, 0)),
            pl.BlockSpec((block_sources, part_rows, hd), lambda i: (i, 0, 0)),
            pl.BlockSpec((nk, hd), lambda i: (0, 0)),
            pl.BlockSpec((nk, hd), lambda i: (0, 0)),
        ],
        out_shape=[
            jax.ShapeDtypeStruct((sources, part_rows, hd), jnp.bfloat16),
            jax.ShapeDtypeStruct((sources, part_rows, hd), jnp.bfloat16),
            jax.ShapeDtypeStruct((nk, hd), jnp.float32),
            jax.ShapeDtypeStruct((nk, hd), jnp.float32),
        ],
        compiler_params=pltpu.CompilerParams(dimension_semantics=("arbitrary",)),
    )(recv, recv, recv, recv, bias.reshape(1, nk))


def per_device(frames, lengths, w_qkv, w_out, cotangent):
    width = w_out.shape[0]
    head_size = width // H
    scale = float(head_size) ** (-0.5)
    tok_rows = frames.shape[1]
    seq_count = lax.axis_size("seq")
    groups = seq_count // H
    part_rows = tok_rows // groups
    frame_total = tok_rows * seq_count
    group_index = lax.axis_index("seq") % groups
    length = lengths[0]
    inputs = frames[0].astype(jnp.float32)
    normed = layer_norm(inputs).astype(jnp.bfloat16)
    qkv = jnp.dot(normed, w_qkv, preferred_element_type=jnp.float32).astype(jnp.bfloat16)
    qkv_local = qkv.reshape(tok_rows, 3, H, head_size)
    offset = lax.axis_index("seq") * tok_rows
    own_pos = offset + jnp.arange(tok_rows, dtype=jnp.int32)
    valid = (own_pos < length).astype(jnp.float32)
    grad_rows = (cotangent[0].astype(jnp.float32) * valid[:, None]).astype(jnp.bfloat16)
    dcontext = jnp.dot(grad_rows, w_out.T, preferred_element_type=jnp.float32).astype(jnp.bfloat16)

    def by_half(rows_heads):
        return rows_heads.reshape(groups, part_rows, H, head_size).transpose(2, 0, 1, 3).reshape(
            seq_count, part_rows, head_size
        )

    def to_both(rows_heads):
        both = jnp.broadcast_to(rows_heads.transpose(1, 0, 2)[:, None], (H, groups, tok_rows, head_size))
        return both.reshape(seq_count, tok_rows, head_size)

    send = jnp.concatenate(
        [
            by_half(qkv_local[:, 0]),
            by_half(dcontext.reshape(tok_rows, H, head_size)),
            to_both(qkv_local[:, 1]),
            to_both(qkv_local[:, 2]),
        ],
        axis=1,
    )
    recv = lax.all_to_all(send, "seq", split_axis=0, concat_axis=0, tiled=True)
    normed_send = jnp.broadcast_to(normed.reshape(1, groups, part_rows, width), (H, groups, part_rows, width))
    normed_recv = lax.all_to_all(
        normed_send.reshape(seq_count, part_rows, width), "seq", split_axis=0, concat_axis=0, tiled=True
    )
    position = jnp.arange(frame_total, dtype=jnp.int32)
    bias = jnp.where(position < length, 0.0, -1000000000.0).astype(jnp.float32)

    context_h, dquery, dkeys, dvalues = attn_pass(recv, part_rows, bias, scale)

    split_grads = jnp.stack([dkeys, dvalues], axis=1).reshape(seq_count, groups, part_rows, 2, head_size)
    own_half = lax.dynamic_index_in_dim(split_grads, group_index, 1, keepdims=False)
    other_half = lax.dynamic_index_in_dim(split_grads, 1 - group_index, 1, keepdims=False)
    partner_half = from_partner(other_half.astype(jnp.bfloat16), "seq", 0)
    paired_rows = (own_half + partner_half.astype(jnp.float32)).astype(jnp.bfloat16)
    back = jnp.concatenate(
        [
            context_h.reshape(seq_count, part_rows, 1, head_size),
            dquery.reshape(seq_count, part_rows, 1, head_size),
            paired_rows,
        ],
        axis=2,
    )
    returned = lax.all_to_all(back, "seq", split_axis=0, concat_axis=0, tiled=True)
    returned = returned.reshape(H, groups, part_rows, 4, head_size).transpose(1, 2, 3, 0, 4)
    context = returned[:, :, 0].reshape(tok_rows, width)
    dqkv = returned[:, :, 1:].reshape(tok_rows, 3 * width)
    branch = jnp.dot(context, w_out, preferred_element_type=jnp.float32)
    output = (inputs + valid[:, None] * branch).astype(jnp.bfloat16)
    over_frames = (((0, 1), (0, 1)), ((), ()))
    qkv_part = lax.dot_general(
        normed_recv, back[:, :, 1:], over_frames, preferred_element_type=jnp.float32
    ).reshape(width, 3 * head_size)
    out_part = jnp.dot(context.T, grad_rows, preferred_element_type=jnp.float32)
    y_count = lax.axis_size("y")
    core_count = lax.axis_size("core")
    core_index = lax.axis_index("core")
    piece_rows = width // (seq_count * y_count * core_count)
    parts = jnp.concatenate([qkv_part, out_part], axis=1).astype(jnp.bfloat16)
    parts = parts.reshape(seq_count, y_count, core_count, piece_rows, parts.shape[1])
    own = lax.dynamic_index_in_dim(parts, core_index, 2, keepdims=False)
    other = lax.dynamic_index_in_dim(parts, 1 - core_index, 2, keepdims=False)
    from_core = lax.ppermute(other, "core", [(0, 1), (1, 0)])
    chip_sum = (own.astype(jnp.float32) + from_core.astype(jnp.float32)).astype(jnp.bfloat16)
    gathered = lax.all_to_all(
        chip_sum.reshape(seq_count * y_count, piece_rows, parts.shape[-1]),
        ("seq", "y"),
        split_axis=0,
        concat_axis=0,
        tiled=True,
    )
    qkv_in = gathered[:, :, : 3 * head_size].astype(jnp.float32)
    qkv_in = jnp.sum(qkv_in.reshape(H, groups * y_count, piece_rows, 3 * head_size), axis=1)
    qkv_rows = qkv_in.reshape(H, piece_rows, 3, head_size).transpose(1, 2, 0, 3).reshape(piece_rows, 3 * width)
    out_rows = jnp.sum(gathered[:, :, 3 * head_size :].astype(jnp.float32), axis=0)
    summed = lax.all_gather(jnp.concatenate([qkv_rows, out_rows], axis=1), ("y", "core"), axis=0, tiled=True)
    grad_qkv = summed[:, : 3 * width]
    grad_out = summed[:, 3 * width :]
    dnormed = jnp.dot(dqkv, w_qkv.T, preferred_element_type=jnp.float32)
    unused, pull = jax.vjp(layer_norm, inputs)
    grad_input = (cotangent[0].astype(jnp.float32) + pull(dnormed)[0]).astype(jnp.bfloat16)
    return (output[None], grad_input[None], grad_qkv, grad_out)


def solution(mesh):
    batch_size = mesh.shape["batch"]
    fine = Mesh(mesh.devices.reshape(batch_size // 2, 2, mesh.shape["seq"]), ("y", "core", "seq"))
    batch = ("y", "core")
    return jax.shard_map(
        per_device,
        mesh=fine,
        in_specs=(P(batch, "seq", None), P(batch), P(), P(), P(batch, "seq", None)),
        out_specs=(
            P(batch, "seq", None),
            P(batch, "seq", None),
            P("seq", None),
            P("seq", None),
        ),
        check_vma=False,
    )
```

```python
import jax
import jax.numpy as jnp
from jax import lax
from jax.sharding import Mesh, PartitionSpec as P
from jax.experimental import pallas as pl
from jax.experimental.pallas import tpu as pltpu
import functools

H = 8


def from_partner(array, axis, stride):
    return lax.ppermute(array, axis, [(i, i ^ 1 << stride) for i in range(lax.axis_size(axis))])


def layer_norm(values):
    mean = jnp.mean(values, axis=-1, keepdims=True)
    centred = values - mean
    var = jnp.mean(centred * centred, axis=-1, keepdims=True)
    return centred * lax.rsqrt(var + 1e-05)


def _attn_kernel(q_ref, do_ref, k_ref, v_ref, bias_ref, ctx_ref, dq_ref, dk_ref, dv_ref, *, scale):
    i = pl.program_id(0)

    @pl.when(i == 0)
    def _():
        dk_ref[...] = jnp.zeros_like(dk_ref)
        dv_ref[...] = jnp.zeros_like(dv_ref)

    nb, rows, hd = q_ref.shape
    ns, kr, _ = k_ref.shape
    q = q_ref[...].reshape(nb * rows, hd)
    do = do_ref[...].reshape(nb * rows, hd)
    k = k_ref[...].reshape(ns * kr, hd)
    v = v_ref[...].reshape(ns * kr, hd)
    nt = (((1,), (1,)), ((), ()))
    tn = (((0,), (0,)), ((), ()))
    s = lax.dot_general(q, k, nt, preferred_element_type=jnp.float32) * scale + bias_ref[...]
    m = jnp.max(s, axis=1, keepdims=True)
    e = jnp.exp(s - m)
    p = e / jnp.sum(e, axis=1, keepdims=True)
    p16 = p.astype(jnp.bfloat16)
    ctx = jnp.dot(p16, v, preferred_element_type=jnp.float32)
    ctx_ref[...] = ctx.reshape(nb, rows, hd).astype(ctx_ref.dtype)
    dp = lax.dot_general(do, v, nt, preferred_element_type=jnp.float32)
    delta = jnp.sum(p * dp, axis=1, keepdims=True)
    ds = (p * (dp - delta)).astype(jnp.bfloat16)
    dq = jnp.dot(ds, k, preferred_element_type=jnp.float32) * scale
    dq_ref[...] = dq.reshape(nb, rows, hd).astype(dq_ref.dtype)
    dk_ref[...] += lax.dot_general(ds, q, tn, preferred_element_type=jnp.float32) * scale
    dv_ref[...] += lax.dot_general(p16, do, tn, preferred_element_type=jnp.float32)


def attn_pass(recv, part_rows, bias, scale, block_sources=4):
    sources, _, hd = recv.shape
    key_rows = 2 * part_rows
    nq = sources * part_rows
    nk = sources * key_rows
    kernel = functools.partial(_attn_kernel, scale=scale)
    return pl.pallas_call(
        kernel,
        grid=(sources // block_sources,),
        in_specs=[
            pl.BlockSpec((block_sources, part_rows, hd), lambda i: (i, 0, 0)),
            pl.BlockSpec((block_sources, part_rows, hd), lambda i: (i, 1, 0)),
            pl.BlockSpec((sources, key_rows, hd), lambda i: (0, 1, 0)),
            pl.BlockSpec((sources, key_rows, hd), lambda i: (0, 2, 0)),
            pl.BlockSpec((1, nk), lambda i: (0, 0)),
        ],
        out_specs=[
            pl.BlockSpec((block_sources, part_rows, hd), lambda i: (i, 0, 0)),
            pl.BlockSpec((block_sources, part_rows, hd), lambda i: (i, 0, 0)),
            pl.BlockSpec((nk, hd), lambda i: (0, 0)),
            pl.BlockSpec((nk, hd), lambda i: (0, 0)),
        ],
        out_shape=[
            jax.ShapeDtypeStruct((sources, part_rows, hd), jnp.bfloat16),
            jax.ShapeDtypeStruct((sources, part_rows, hd), jnp.bfloat16),
            jax.ShapeDtypeStruct((nk, hd), jnp.float32),
            jax.ShapeDtypeStruct((nk, hd), jnp.float32),
        ],
        compiler_params=pltpu.CompilerParams(dimension_semantics=("arbitrary",)),
    )(recv, recv, recv, recv, bias.reshape(1, nk))


def per_device(frames, lengths, w_qkv, w_out, cotangent):
    width = w_out.shape[0]
    head_size = width // H
    scale = float(head_size) ** (-0.5)
    tok_rows = frames.shape[1]
    seq_count = lax.axis_size("seq")
    groups = seq_count // H
    part_rows = tok_rows // groups
    frame_total = tok_rows * seq_count
    group_index = lax.axis_index("seq") % groups
    length = lengths[0]
    inputs = frames[0].astype(jnp.float32)
    normed = layer_norm(inputs).astype(jnp.bfloat16)
    qkv = jnp.dot(normed, w_qkv, preferred_element_type=jnp.float32).astype(jnp.bfloat16)
    qkv_local = qkv.reshape(tok_rows, 3, H, head_size)
    offset = lax.axis_index("seq") * tok_rows
    own_pos = offset + jnp.arange(tok_rows, dtype=jnp.int32)
    valid = (own_pos < length).astype(jnp.float32)
    grad_rows = (cotangent[0].astype(jnp.float32) * valid[:, None]).astype(jnp.bfloat16)
    dcontext = jnp.dot(grad_rows, w_out.T, preferred_element_type=jnp.float32).astype(jnp.bfloat16)

    def by_half(rows_heads):
        return rows_heads.reshape(groups, part_rows, H, head_size).transpose(2, 0, 1, 3).reshape(
            seq_count, part_rows, head_size
        )

    def to_both(rows_heads):
        both = jnp.broadcast_to(rows_heads.transpose(1, 0, 2)[:, None], (H, groups, tok_rows, head_size))
        return both.reshape(seq_count, tok_rows, head_size)

    send = jnp.concatenate(
        [
            by_half(qkv_local[:, 0]),
            by_half(dcontext.reshape(tok_rows, H, head_size)),
            to_both(qkv_local[:, 1]),
            to_both(qkv_local[:, 2]),
        ],
        axis=1,
    )
    recv = lax.all_to_all(send, "seq", split_axis=0, concat_axis=0, tiled=True)
    normed_send = jnp.broadcast_to(normed.reshape(1, groups, part_rows, width), (H, groups, part_rows, width))
    normed_recv = lax.all_to_all(
        normed_send.reshape(seq_count, part_rows, width), "seq", split_axis=0, concat_axis=0, tiled=True
    )
    position = jnp.arange(frame_total, dtype=jnp.int32)
    bias = jnp.where(position < length, 0.0, -1000000000.0).astype(jnp.float32)

    context_h, dquery, dkeys, dvalues = attn_pass(recv, part_rows, bias, scale)

    split_grads = jnp.stack([dkeys, dvalues], axis=1).reshape(seq_count, groups, part_rows, 2, head_size)
    own_half = lax.dynamic_index_in_dim(split_grads, group_index, 1, keepdims=False)
    other_half = lax.dynamic_index_in_dim(split_grads, 1 - group_index, 1, keepdims=False)
    partner_half = from_partner(other_half.astype(jnp.bfloat16), "seq", 0)
    paired_rows = (own_half + partner_half.astype(jnp.float32)).astype(jnp.bfloat16)
    back = jnp.concatenate(
        [
            context_h.reshape(seq_count, part_rows, 1, head_size),
            dquery.reshape(seq_count, part_rows, 1, head_size),
            paired_rows,
        ],
        axis=2,
    )
    returned = lax.all_to_all(back, "seq", split_axis=0, concat_axis=0, tiled=True)
    returned_heads = returned.reshape(H, groups, part_rows, 4, head_size)
    returned = returned_heads.transpose(1, 2, 3, 0, 4)
    context = returned[:, :, 0].reshape(tok_rows, width)
    dqkv = returned[:, :, 1:].reshape(tok_rows, 3 * width)
    branch = jnp.dot(context, w_out, preferred_element_type=jnp.float32)
    output = (inputs + valid[:, None] * branch).astype(jnp.bfloat16)
    over_frames = (((0, 1), (0, 1)), ((), ()))
    qkv_part = lax.dot_general(
        normed_recv, back[:, :, 1:], over_frames, preferred_element_type=jnp.float32
    ).reshape(width, 3 * head_size)
    out_part = jnp.dot(context.T, grad_rows, preferred_element_type=jnp.float32)
    y_count = lax.axis_size("y")
    core_count = lax.axis_size("core")
    core_index = lax.axis_index("core")
    piece_rows = width // (seq_count * y_count * core_count)
    parts = jnp.concatenate([qkv_part, out_part], axis=1).astype(jnp.bfloat16)
    parts = parts.reshape(seq_count, y_count, core_count, piece_rows, parts.shape[1])
    own = lax.dynamic_index_in_dim(parts, core_index, 2, keepdims=False)
    other = lax.dynamic_index_in_dim(parts, 1 - core_index, 2, keepdims=False)
    from_core = lax.ppermute(other, "core", [(0, 1), (1, 0)])
    chip_sum = (own.astype(jnp.float32) + from_core.astype(jnp.float32)).astype(jnp.bfloat16)
    gathered = lax.all_to_all(
        chip_sum.reshape(seq_count * y_count, piece_rows, parts.shape[-1]),
        ("seq", "y"),
        split_axis=0,
        concat_axis=0,
        tiled=True,
    )
    qkv_in = gathered[:, :, : 3 * head_size].astype(jnp.float32)
    qkv_in = jnp.sum(qkv_in.reshape(H, groups * y_count, piece_rows, 3 * head_size), axis=1)
    qkv_rows = qkv_in.reshape(H, piece_rows, 3, head_size).transpose(1, 2, 0, 3).reshape(piece_rows, 3 * width)
    out_rows = jnp.sum(gathered[:, :, 3 * head_size :].astype(jnp.float32), axis=0)
    summed = lax.all_gather(jnp.concatenate([qkv_rows, out_rows], axis=1), ("y", "core"), axis=0, tiled=True)
    grad_qkv = summed[:, : 3 * width]
    grad_out = summed[:, 3 * width :]
    dnormed = lax.dot_general(
        returned_heads[:, :, :, 1:],
        w_qkv.reshape(width, 3, H, head_size),
        (((0, 3, 4), (2, 1, 3)), ((), ())),
        preferred_element_type=jnp.float32,
    ).reshape(tok_rows, width)
    unused, pull = jax.vjp(layer_norm, inputs)
    grad_input = (cotangent[0].astype(jnp.float32) + pull(dnormed)[0]).astype(jnp.bfloat16)
    return (output[None], grad_input[None], grad_qkv, grad_out)


def solution(mesh):
    batch_size = mesh.shape["batch"]
    fine = Mesh(mesh.devices.reshape(batch_size // 2, 2, mesh.shape["seq"]), ("y", "core", "seq"))
    batch = ("y", "core")
    return jax.shard_map(
        per_device,
        mesh=fine,
        in_specs=(P(batch, "seq", None), P(batch), P(), P(), P(batch, "seq", None)),
        out_specs=(
            P(batch, "seq", None),
            P(batch, "seq", None),
            P("seq", None),
            P("seq", None),
        ),
        check_vma=False,
    )
```

```python
import jax
import jax.numpy as jnp
from jax import lax
from jax.sharding import Mesh, PartitionSpec as P
from jax.experimental import pallas as pl
from jax.experimental.pallas import tpu as pltpu
import functools

H = 8


def from_partner(array, axis, stride):
    return lax.ppermute(array, axis, [(i, i ^ 1 << stride) for i in range(lax.axis_size(axis))])


def layer_norm(values):
    mean = jnp.mean(values, axis=-1, keepdims=True)
    centred = values - mean
    var = jnp.mean(centred * centred, axis=-1, keepdims=True)
    return centred * lax.rsqrt(var + 1e-05)


def _attn_kernel(q_ref, do_ref, k_ref, v_ref, bias_ref, ctx_ref, dq_ref, dk_ref, dv_ref, *, scale):
    i = pl.program_id(0)

    @pl.when(i == 0)
    def _():
        dk_ref[...] = jnp.zeros_like(dk_ref)
        dv_ref[...] = jnp.zeros_like(dv_ref)

    nb, rows, hd = q_ref.shape
    ns, kr, _ = k_ref.shape
    q = q_ref[...].reshape(nb * rows, hd)
    do = do_ref[...].reshape(nb * rows, hd)
    k = k_ref[...].reshape(ns * kr, hd)
    v = v_ref[...].reshape(ns * kr, hd)
    nt = (((1,), (1,)), ((), ()))
    tn = (((0,), (0,)), ((), ()))
    s = lax.dot_general(q, k, nt, preferred_element_type=jnp.float32) * scale + bias_ref[...]
    m = jnp.max(s, axis=1, keepdims=True)
    e = jnp.exp(s - m)
    p = e / jnp.sum(e, axis=1, keepdims=True)
    p16 = p.astype(jnp.bfloat16)
    ctx = jnp.dot(p16, v, preferred_element_type=jnp.float32)
    ctx_ref[...] = ctx.reshape(nb, rows, hd).astype(ctx_ref.dtype)
    dp = lax.dot_general(do, v, nt, preferred_element_type=jnp.float32)
    delta = jnp.sum(p * dp, axis=1, keepdims=True)
    ds = (p * (dp - delta)).astype(jnp.bfloat16)
    dq = jnp.dot(ds, k, preferred_element_type=jnp.float32) * scale
    dq_ref[...] = dq.reshape(nb, rows, hd).astype(dq_ref.dtype)
    dk_ref[...] += lax.dot_general(ds, q, tn, preferred_element_type=jnp.float32) * scale
    dv_ref[...] += lax.dot_general(p16, do, tn, preferred_element_type=jnp.float32)


def attn_pass(recv, part_rows, bias, scale, block_sources=4):
    sources, _, hd = recv.shape
    key_rows = 2 * part_rows
    nq = sources * part_rows
    nk = sources * key_rows
    kernel = functools.partial(_attn_kernel, scale=scale)
    return pl.pallas_call(
        kernel,
        grid=(sources // block_sources,),
        in_specs=[
            pl.BlockSpec((block_sources, part_rows, hd), lambda i: (i, 0, 0)),
            pl.BlockSpec((block_sources, part_rows, hd), lambda i: (i, 1, 0)),
            pl.BlockSpec((sources, key_rows, hd), lambda i: (0, 1, 0)),
            pl.BlockSpec((sources, key_rows, hd), lambda i: (0, 2, 0)),
            pl.BlockSpec((1, nk), lambda i: (0, 0)),
        ],
        out_specs=[
            pl.BlockSpec((block_sources, part_rows, hd), lambda i: (i, 0, 0)),
            pl.BlockSpec((block_sources, part_rows, hd), lambda i: (i, 0, 0)),
            pl.BlockSpec((nk, hd), lambda i: (0, 0)),
            pl.BlockSpec((nk, hd), lambda i: (0, 0)),
        ],
        out_shape=[
            jax.ShapeDtypeStruct((sources, part_rows, hd), jnp.bfloat16),
            jax.ShapeDtypeStruct((sources, part_rows, hd), jnp.bfloat16),
            jax.ShapeDtypeStruct((nk, hd), jnp.float32),
            jax.ShapeDtypeStruct((nk, hd), jnp.float32),
        ],
        compiler_params=pltpu.CompilerParams(dimension_semantics=("arbitrary",)),
    )(recv, recv, recv, recv, bias.reshape(1, nk))


def per_device(frames, lengths, w_qkv, w_out, cotangent):
    width = w_out.shape[0]
    head_size = width // H
    scale = float(head_size) ** (-0.5)
    tok_rows = frames.shape[1]
    seq_count = lax.axis_size("seq")
    groups = seq_count // H
    part_rows = tok_rows // groups
    frame_total = tok_rows * seq_count
    group_index = lax.axis_index("seq") % groups
    length = lengths[0]
    inputs = frames[0].astype(jnp.float32)
    normed = layer_norm(inputs).astype(jnp.bfloat16)
    qkv = jnp.dot(normed, w_qkv, preferred_element_type=jnp.float32).astype(jnp.bfloat16)
    qkv_local = qkv.reshape(tok_rows, 3, H, head_size)
    offset = lax.axis_index("seq") * tok_rows
    own_pos = offset + jnp.arange(tok_rows, dtype=jnp.int32)
    valid = (own_pos < length).astype(jnp.float32)
    grad_rows = (cotangent[0].astype(jnp.float32) * valid[:, None]).astype(jnp.bfloat16)
    dcontext = jnp.dot(grad_rows, w_out.T, preferred_element_type=jnp.float32).astype(jnp.bfloat16)

    def by_half(rows_heads):
        return rows_heads.reshape(groups, part_rows, H, head_size).transpose(2, 0, 1, 3).reshape(
            seq_count, part_rows, head_size
        )

    def to_both(rows_heads):
        both = jnp.broadcast_to(rows_heads.transpose(1, 0, 2)[:, None], (H, groups, tok_rows, head_size))
        return both.reshape(seq_count, tok_rows, head_size)

    send = jnp.concatenate(
        [
            by_half(qkv_local[:, 0]),
            by_half(dcontext.reshape(tok_rows, H, head_size)),
            to_both(qkv_local[:, 1]),
            to_both(qkv_local[:, 2]),
        ],
        axis=1,
    )
    recv = lax.all_to_all(send, "seq", split_axis=0, concat_axis=0, tiled=True)
    normed_send = jnp.broadcast_to(normed.reshape(1, groups, part_rows, width), (H, groups, part_rows, width))
    normed_recv = lax.all_to_all(
        normed_send.reshape(seq_count, part_rows, width), "seq", split_axis=0, concat_axis=0, tiled=True
    )
    position = jnp.arange(frame_total, dtype=jnp.int32)
    bias = jnp.where(position < length, 0.0, -1000000000.0).astype(jnp.float32)

    context_h, dquery, dkeys, dvalues = attn_pass(recv, part_rows, bias, scale)

    split_grads = jnp.stack([dkeys, dvalues], axis=1).reshape(seq_count, groups, part_rows, 2, head_size)
    own_half = lax.dynamic_index_in_dim(split_grads, group_index, 1, keepdims=False)
    other_half = lax.dynamic_index_in_dim(split_grads, 1 - group_index, 1, keepdims=False)
    partner_half = from_partner(other_half.astype(jnp.bfloat16), "seq", 0)
    paired_rows = (own_half + partner_half.astype(jnp.float32)).astype(jnp.bfloat16)
    back = jnp.concatenate(
        [
            context_h.reshape(seq_count, part_rows, 1, head_size),
            dquery.reshape(seq_count, part_rows, 1, head_size),
            paired_rows,
        ],
        axis=2,
    )
    returned = lax.all_to_all(back, "seq", split_axis=0, concat_axis=0, tiled=True)
    returned_heads = returned.reshape(H, groups, part_rows, 4, head_size)
    context_heads = returned_heads[:, :, :, 0]
    branch = lax.dot_general(
        context_heads, w_out.reshape(H, head_size, width), (((0, 3), (0, 1)), ((), ())),
        preferred_element_type=jnp.float32,
    ).reshape(tok_rows, width)
    output = (inputs + valid[:, None] * branch).astype(jnp.bfloat16)
    over_frames = (((0, 1), (0, 1)), ((), ()))
    qkv_part = lax.dot_general(
        normed_recv, back[:, :, 1:], over_frames, preferred_element_type=jnp.float32
    ).reshape(width, 3 * head_size)
    out_part = lax.dot_general(
        context_heads, grad_rows.reshape(groups, part_rows, width), (((1, 2), (0, 1)), ((), ())),
        preferred_element_type=jnp.float32,
    ).reshape(width, width)
    y_count = lax.axis_size("y")
    core_count = lax.axis_size("core")
    core_index = lax.axis_index("core")
    piece_rows = width // (seq_count * y_count * core_count)
    parts = jnp.concatenate([qkv_part, out_part], axis=1).astype(jnp.bfloat16)
    parts = parts.reshape(seq_count, y_count, core_count, piece_rows, parts.shape[1])
    own = lax.dynamic_index_in_dim(parts, core_index, 2, keepdims=False)
    other = lax.dynamic_index_in_dim(parts, 1 - core_index, 2, keepdims=False)
    from_core = lax.ppermute(other, "core", [(0, 1), (1, 0)])
    chip_sum = (own.astype(jnp.float32) + from_core.astype(jnp.float32)).astype(jnp.bfloat16)
    gathered = lax.all_to_all(
        chip_sum.reshape(seq_count * y_count, piece_rows, parts.shape[-1]),
        ("seq", "y"),
        split_axis=0,
        concat_axis=0,
        tiled=True,
    )
    qkv_in = gathered[:, :, : 3 * head_size].astype(jnp.float32)
    qkv_in = jnp.sum(qkv_in.reshape(H, groups * y_count, piece_rows, 3 * head_size), axis=1)
    qkv_rows = qkv_in.reshape(H, piece_rows, 3, head_size).transpose(1, 2, 0, 3).reshape(piece_rows, 3 * width)
    out_rows = jnp.sum(gathered[:, :, 3 * head_size :].astype(jnp.float32), axis=0)
    summed = lax.all_gather(jnp.concatenate([qkv_rows, out_rows], axis=1), ("y", "core"), axis=0, tiled=True)
    grad_qkv = summed[:, : 3 * width]
    grad_out = summed[:, 3 * width :]
    dnormed = lax.dot_general(
        returned_heads[:, :, :, 1:],
        w_qkv.reshape(width, 3, H, head_size),
        (((0, 3, 4), (2, 1, 3)), ((), ())),
        preferred_element_type=jnp.float32,
    ).reshape(tok_rows, width)
    unused, pull = jax.vjp(layer_norm, inputs)
    grad_input = (cotangent[0].astype(jnp.float32) + pull(dnormed)[0]).astype(jnp.bfloat16)
    return (output[None], grad_input[None], grad_qkv, grad_out)


def solution(mesh):
    batch_size = mesh.shape["batch"]
    fine = Mesh(mesh.devices.reshape(batch_size // 2, 2, mesh.shape["seq"]), ("y", "core", "seq"))
    batch = ("y", "core")
    return jax.shard_map(
        per_device,
        mesh=fine,
        in_specs=(P(batch, "seq", None), P(batch), P(), P(), P(batch, "seq", None)),
        out_specs=(
            P(batch, "seq", None),
            P(batch, "seq", None),
            P("seq", None),
            P("seq", None),
        ),
        check_vma=False,
    )
```
